512 devices in a mesh: req: 32 (over y, x, core), grp: 16 (over z).
Axes of the slice: x: 4, y: 4, z: 16, core: 2. Of those that a mesh axis runs over, the one named last changes fastest.
Arguments:
- normed_token_input: bfloat16 [256, 8192], P(None, 'req'), may hold values from -6 to 6
- key_value_weight: bfloat16 [8192, 2048], P('req', 'grp'), may hold values from -0.0625 to 0.0625
- adapter_down_weight: bfloat16 [8192, 128, 128], P('req', 'grp'), may hold values from -0.0625 to 0.0625
- adapter_up_weight: bfloat16 [128, 64, 2048], P(None, None, 'grp'), may hold values from -0.75 to 0.75
- adapter_index_rows: int32 [256, 1], replicated, may hold values from 0 to 127
- queries: bfloat16 [256, 8192], P('req')
- key_value_pages: bfloat16 [10240, 16, 2, 8, 128], P('req', 'grp')
- lengths: int32 [256], P('req'), may hold values from 0 to 511, as said below
- page_slot_table: int32 [256, 32], P('req'), may hold values from 0 to 255, as said below
- departing_slots: int32 [1024], P('req'), may hold values from 0 to 255, as said below
- departing_target: int32 [1024, 1], P('req'), may hold values from 0 to 31; in each aligned block of 32 rows (0 to 31, 32 to 63, ...) at most 2 rows name the same one
Outputs:
- attention: bfloat16 [256, 8192], P('req')
- migrated_pool: bfloat16 [10240, 16, 2, 8, 128], P('req', 'grp')
The draws below stay inside these ranges and needn't reach their ends.
Inputs may be any that keep to these rules, and one draw needn't show every extreme that they name: `adapter_index_rows`: each row names one adapter; every adapter is named by some request. `lengths`: some request has an empty cache and some has 511 cached tokens. `page_slot_table`: the rows of the requests of one home together name each of that home's slots 0 .. 255 exactly once. `departing_slots`: the 32 entries of one home are distinct. `departing_target`: the 32 rows of one home name one target at most 2 times; some home names some target exactly 2 times.
All inputs are finite; a program needn't handle non-finite values.
Results may differ from the reference program's by a relative error of at most 0.01345.
Values may be sent and summed in bfloat16 or wider, within the bound.
No kernel may reach another device: no remote copies, remote signals or barrier semaphores. Data moves between devices by JAX's collectives and lax.ppermute only.
A program may use at most 64 MiB of HBM per device.

```python
import math
import jax
import jax.numpy as jnp
import numpy as np
from jax import lax

MODEL_WIDTH = 8192
KEY_VALUE_HEADS = 8
GQ = 8
HEAD_SIZE = 128
ADAPTER_RANK = 64
PAGE = 16
REQ_DEV = 8
MAXP = 32
MIG_DEV = 32
HOMES = 32
REQUEST_COUNT = 256
ADAPTER_COUNT = 128
CAP = 2
LIVE = 256
POOL_DEV = 320
POOL_ALL = 10240


def shared_direction(key):
    signs = jax.random.bernoulli(jax.random.fold_in(key, 91), 0.5, (KEY_VALUE_HEADS, HEAD_SIZE))
    return 2.0 * signs.astype(jnp.float32) - 1.0


def local_orders(key, count):
    keys = jax.random.split(key, HOMES)
    return jax.vmap(lambda single: jax.random.permutation(single, count))(keys)


def base_noise(key, shape):
    return jax.random.normal(key, shape, jnp.float32)


def draw_queries(key, part):
    noise = base_noise(jax.random.fold_in(key, 1), (REQUEST_COUNT, KEY_VALUE_HEADS, GQ, HEAD_SIZE))
    aligned = jax.random.bernoulli(jax.random.fold_in(key, 2), 0.25, (REQUEST_COUNT, 1, 1, 1)).astype(jnp.float32)
    first = (jnp.arange(REQUEST_COUNT) == 0).astype(jnp.float32)[:, None, None, None]
    aligned = jnp.maximum(aligned, first)
    strength = jax.random.uniform(jax.random.fold_in(key, 10), (REQUEST_COUNT, KEY_VALUE_HEADS, GQ, 1), jnp.float32, 4.0, 24.0)
    mixed = noise * (1.0 - 0.7 * aligned) + aligned * strength * shared_direction(key)[None, :, None, :]
    return mixed.reshape(REQUEST_COUNT, KEY_VALUE_HEADS * GQ * HEAD_SIZE).astype(jnp.bfloat16)


def draw_key_value_pages(key, part):
    noise = base_noise(jax.random.fold_in(key, 3), (POOL_ALL, PAGE, 2, KEY_VALUE_HEADS, HEAD_SIZE))
    strength = jax.random.uniform(jax.random.fold_in(key, 4), (POOL_ALL, PAGE, 1, KEY_VALUE_HEADS, 1), jnp.float32, 0.0, 2.5)
    is_key = (jnp.arange(2) == 0).astype(jnp.float32)[None, None, :, None, None]
    mixed = noise * (1.0 - 0.4 * is_key) + is_key * strength * shared_direction(key)[None, None, None, :, :]
    return mixed.astype(jnp.bfloat16)


def draw_lengths(key, part):
    total = MAXP * PAGE
    limits = jax.random.randint(jax.random.fold_in(key, 5), (HOMES, 1), total // 4, total + 1)
    drawn = jax.random.randint(jax.random.fold_in(key, 6), (HOMES, REQ_DEV), 0, limits).reshape(REQUEST_COUNT)
    picks = jax.random.permutation(jax.random.fold_in(key, 7), REQUEST_COUNT)
    return drawn.at[picks[0]].set(total - 1).at[picks[1]].set(0).astype(jnp.int32)


def draw_page_slot_table(key, part):
    return local_orders(jax.random.fold_in(key, 8), LIVE).reshape(REQUEST_COUNT, MAXP).astype(jnp.int32)


def draw_departing_slots(key, part):
    return local_orders(jax.random.fold_in(key, 9), LIVE)[:, :MIG_DEV].reshape(HOMES * MIG_DEV).astype(jnp.int32)


def with_spikes(entries, key, source, target, blocks, factor):
    owner, partner = [(jnp.arange(entries.shape[position]) // (entries.shape[position] // blocks)).reshape([-1 if axis == position else 1 for axis in range(entries.ndim)]) for position in (source, target)]
    chosen = jax.random.permutation(key, blocks)[partner]
    strong = (owner == chosen) | (owner == (partner + blocks // 2) % blocks)
    return jnp.where(strong, factor * entries, entries)


def levels(rng, shape, shards, smallest, top_value):
    factor_of = 1.0
    for dim, shards_of in shards:
        steps = jax.random.uniform(jax.random.fold_in(jax.random.fold_in(rng, 6), dim), (shards_of,), jnp.float32, smallest / len(shards), top_value / len(shards))
        factor_of = factor_of * jnp.repeat(jnp.exp(steps), shape[dim] // shards_of).reshape((-1,) + (1,) * (len(shape) - 1 - dim))
    return factor_of


def distinct(own_key, rows, amount, top, lift):
    order = jax.random.permutation(jax.random.fold_in(own_key, 1), amount)
    favour = order
    for power in range(3):
        favour = favour * favour // amount
    favour = favour * lift // amount
    chance = jax.random.randint(jax.random.fold_in(own_key, 2), (rows, amount), 0, 4096) + favour
    sure = jax.random.permutation(jax.random.fold_in(own_key, 3), rows)[jnp.arange(amount) % rows]
    chance = jnp.where(jnp.arange(rows)[:, None] == sure[None, :], 1 << 14, chance)
    score = chance * amount + jnp.arange(amount)
    return lax.top_k(score.astype(jnp.int32), top)[1].astype(jnp.int32)


def routed_block(rng, own, number, rows, amount, top, limit, skew):
    order = jax.random.permutation(rng, amount)
    packed, usual = load_shares(amount, rows * top, limit, skew, True), load_shares(amount, rows * top, limit, skew, False)
    places = jnp.arange(amount)

    def named(sizes, rotation):
        used = int((sizes > 0).sum())
        fixed = max(1, used // 4)
        passed = fixed + (places - fixed + rotation * (used - fixed)) % max(1, amount - fixed)
        return jnp.zeros((amount,), jnp.int32).at[order[jnp.where(places < fixed, places, passed)]].set(jnp.asarray(sizes, jnp.int32))

    sizes = jnp.where(number % 4 == 0, named(packed, number // 4), named(usual, number - number // 4 - 1))
    mixed = jax.random.permutation(jax.random.fold_in(own, 3), amount)
    giver, sink = mixed[0:amount // 2 * 2:2], mixed[1:amount // 2 * 2:2]
    margin = jnp.minimum(sizes[giver] - 1, limit - sizes[sink]) // 2
    margin = jnp.where((giver == order[0]) | (sink == order[0]) | (sizes[sink] == 0), 0, jnp.maximum(margin, 0))
    passed = jax.random.randint(jax.random.fold_in(own, 4), (amount // 2,), 0, 1 << 20) % (margin + 1)
    sizes = sizes.at[giver].add(-passed).at[sink].add(passed)
    items = jnp.searchsorted(jnp.cumsum(sizes), jnp.arange(rows * top), side="right").astype(jnp.int32)
    grid = items.reshape(top, rows).T
    grid = grid[jax.random.permutation(jax.random.fold_in(own, 1), rows)]
    rotation = jax.random.randint(jax.random.fold_in(own, 2), (rows, 1), 0, top)
    return jnp.take_along_axis(grid, (jnp.arange(top)[None, :] + rotation) % top, axis=1)


def load_shares(number_of, total, most, skew, full):
    portions = [(1 << 20) // math.isqrt(standing ** skew) + 1 for standing in range(1, number_of + 1)]
    largest = most if full else min(most, max(-(-total // number_of), total * portions[0] // sum(portions)))
    least = 1 if total - largest >= number_of - 1 else 0
    given, rest = [largest] + [least] * (number_of - 1), total - largest - least * (number_of - 1)
    while rest > 0:
        free = [i for i in range(1, number_of) if given[i] < largest] or [i for i in range(1, number_of) if given[i] < most]
        whole, budget = sum([portions[i] for i in free]), rest
        for i in free:
            more = min(most - given[i], max(1, budget * portions[i] // whole), rest)
            given[i] = given[i] + more
            rest = rest - more
    return np.array(given)


def bell_draw(own_key, extent, scale, most, shards=(), kind=jnp.bfloat16):
    loudness = levels(own_key, extent, shards, -0.22, 0.18) if shards else 1.0
    result = jax.random.normal(own_key, extent, jnp.float32) * scale * loudness
    return jnp.minimum(jnp.maximum(result, -most), most).astype(kind)


def bell_draw_with(rng, shape, width, most, pieces, heavy, held_as=jnp.bfloat16):
    values = width * jax.random.normal(rng, shape, jnp.float32)
    if pieces:
        values = values * levels(rng, shape, pieces, -0.22, 0.18)
    return jnp.clip(with_spikes(values, jax.random.fold_in(rng, 3), *heavy), -most, most).astype(held_as)


def setup_inputs(seed: int = 0) -> dict:
    arg_keys = jax.random.split(jax.random.key(seed), 12)
    normed_token_input = bell_draw_with(arg_keys[0], (REQUEST_COUNT, MODEL_WIDTH), 1.0, 6.0, ((1, 32),), (1, 0, 32, 2.75))
    key_value_weight = bell_draw(arg_keys[1], (MODEL_WIDTH, 2 * KEY_VALUE_HEADS * HEAD_SIZE), MODEL_WIDTH ** -0.5, 0.0625, ((0, 32), (1, 16)))
    adapter_down_weight = bell_draw(arg_keys[2], (MODEL_WIDTH, ADAPTER_COUNT, 2 * ADAPTER_RANK), MODEL_WIDTH ** -0.5, 0.0625, ((0, 32), (1, 16)))
    adapter_up_weight = bell_draw(arg_keys[3], (ADAPTER_COUNT, ADAPTER_RANK, 2 * KEY_VALUE_HEADS * HEAD_SIZE), ADAPTER_RANK ** -0.5, 0.75, ((2, 16),))
    adapter_index_rows = distinct(arg_keys[4], REQUEST_COUNT, ADAPTER_COUNT, 1, 128)
    queries = draw_queries(jax.random.fold_in(arg_keys[11], 71), 0)
    key_value_pages = draw_key_value_pages(jax.random.fold_in(arg_keys[11], 71), 0)
    lengths = draw_lengths(jax.random.fold_in(arg_keys[11], 71), 0)
    page_slot_table = draw_page_slot_table(jax.random.fold_in(arg_keys[11], 71), 0)
    departing_slots = draw_departing_slots(jax.random.fold_in(arg_keys[11], 71), 0)
    departing_target_keys = jax.random.split(jax.random.fold_in(arg_keys[10], 1), (HOMES * MIG_DEV) // MIG_DEV)
    departing_target_turns = jax.random.permutation(jax.random.fold_in(arg_keys[10], 3), (HOMES * MIG_DEV) // MIG_DEV)
    departing_target = jax.vmap(lambda own, number: routed_block(jax.random.fold_in(arg_keys[10], 2), own, number, MIG_DEV, HOMES, 1, CAP, 2))(departing_target_keys, departing_target_turns).reshape((HOMES * MIG_DEV, 1))
    return dict(normed_token_input=normed_token_input, key_value_weight=key_value_weight, adapter_down_weight=adapter_down_weight, adapter_up_weight=adapter_up_weight, adapter_index_rows=adapter_index_rows, queries=queries, key_value_pages=key_value_pages, lengths=lengths, page_slot_table=page_slot_table, departing_slots=departing_slots, departing_target=departing_target)


adapter_scale = 2.0
masked_score = -1e+30

def reference(normed_token_input, key_value_weight, adapter_down_weight, adapter_up_weight, adapter_index_rows, queries, key_value_pages, lengths, page_slot_table, departing_slots, departing_target):
    selected_adapter = adapter_index_rows[:, 0]
    base_projection = jnp.dot(normed_token_input, key_value_weight, preferred_element_type=jnp.float32)

    def apply_adapter(running, request_position):
        down_product = jnp.dot(normed_token_input, adapter_down_weight[:, request_position, :], preferred_element_type=jnp.float32)
        return (running + jnp.where((selected_adapter == request_position)[:, None], down_product, 0.0), request_position)
    adapter_middle = lax.scan(apply_adapter, jnp.zeros((REQUEST_COUNT, 2 * ADAPTER_RANK), jnp.float32), jnp.arange(ADAPTER_COUNT, dtype=jnp.int32))[0]
    middle_rounded = lax.optimization_barrier(adapter_middle.astype(jnp.bfloat16))
    mid_cast = middle_rounded.astype(jnp.float32)
    up_weight_rows = adapter_up_weight[selected_adapter].astype(jnp.float32)
    key_width = KEY_VALUE_HEADS * HEAD_SIZE
    key_update = jnp.einsum('ir,irc->ic', mid_cast[:, :ADAPTER_RANK], up_weight_rows[:, :, :key_width])
    value_update = jnp.einsum('ir,irc->ic', mid_cast[:, ADAPTER_RANK:], up_weight_rows[:, :, key_width:])
    fresh_key_value = (base_projection + adapter_scale * jnp.concatenate([key_update, value_update], axis=1)).astype(jnp.bfloat16)
    requests = jnp.arange(REQUEST_COUNT, dtype=jnp.int32)
    owners = requests // REQ_DEV
    target_slot = owners * POOL_DEV + page_slot_table[requests, lengths // PAGE]
    offset = lengths % PAGE
    written = key_value_pages.at[target_slot, offset, 0].set(fresh_key_value[:, :key_width].reshape(REQUEST_COUNT, KEY_VALUE_HEADS, HEAD_SIZE))
    written = written.at[target_slot, offset, 1].set(fresh_key_value[:, key_width:].reshape(REQUEST_COUNT, KEY_VALUE_HEADS, HEAD_SIZE))

    def attend(item):
        query, table_row, owner, length = item
        gathered = written[owner * POOL_DEV + table_row]
        keys = gathered[:, :, 0].reshape(MAXP * PAGE, KEY_VALUE_HEADS, HEAD_SIZE).astype(jnp.float32)
        values = gathered[:, :, 1].reshape(MAXP * PAGE, KEY_VALUE_HEADS, HEAD_SIZE).astype(jnp.float32)
        heads_query = query.reshape(KEY_VALUE_HEADS, GQ, HEAD_SIZE).astype(jnp.float32)
        scores = jnp.einsum('hgd,nhd->hgn', heads_query, keys) / math.sqrt(HEAD_SIZE)
        valid = jnp.arange(MAXP * PAGE, dtype=jnp.int32) <= length
        scores = jnp.where(valid, scores, masked_score)
        top = lax.optimization_barrier(jnp.max(scores, axis=2, keepdims=True))
        weights = jnp.where(valid, jnp.exp(scores - top), 0.0)
        mixed = jnp.einsum('hgn,nhd->hgd', weights, values) / lax.optimization_barrier(jnp.sum(weights, axis=2))[..., None]
        return mixed.reshape(KEY_VALUE_HEADS * GQ * HEAD_SIZE).astype(jnp.bfloat16)
    attention = lax.map(attend, (queries, page_slot_table, owners, lengths))
    leaving = departing_slots.reshape(HOMES, MIG_DEV)
    targets = departing_target[:, 0].reshape(HOMES, MIG_DEV)
    order = jnp.arange(MIG_DEV, dtype=jnp.int32)
    earlier = (targets[:, :, None] == targets[:, None, :]) & (order[None, None, :] < order[None, :, None])
    place = lax.optimization_barrier(jnp.sum(earlier.astype(jnp.int32), axis=2))
    sources = jnp.arange(HOMES, dtype=jnp.int32)[:, None]
    from_slot = (sources * POOL_DEV + leaving).reshape(HOMES * MIG_DEV)
    to_slot = (targets * POOL_DEV + LIVE + sources * CAP + place).reshape(HOMES * MIG_DEV)
    is_landing = jnp.arange(POOL_ALL, dtype=jnp.int32) % POOL_DEV >= LIVE
    cleared = jnp.where(is_landing[:, None, None, None, None], jnp.zeros((), written.dtype), written)
    migrated_pool = cleared.at[to_slot].set(written[from_slot])
    return (attention, migrated_pool)
```

```python
import math

import jax
import jax.numpy as jnp
from jax import lax
from jax.sharding import PartitionSpec as P

adapter_scale = 2.0
masked_score = -1e30


def shards(
    normed_token_input,
    key_value_weight,
    adapter_down_weight,
    adapter_up_weight,
    adapter_index_rows,
    queries,
    key_value_pages,
    lengths,
    page_slot_table,
    departing_slots,
    departing_target,
):
    selected_adapter = adapter_index_rows[:, 0]
    homes = lax.axis_size("req")
    groups = lax.axis_size("grp")
    home_index = lax.axis_index("req")
    group_index = lax.axis_index("grp")
    rows = lengths.shape[0]
    request_count = normed_token_input.shape[0]
    column_span = key_value_weight.shape[1]
    local_adapters = adapter_down_weight.shape[1]
    rank_width = adapter_down_weight.shape[2]
    rank_half = adapter_up_weight.shape[1]
    slot_tokens = key_value_pages.shape[1]
    heads = key_value_pages.shape[3]
    head_dim = key_value_pages.shape[4]
    key_width = heads * head_dim
    query_heads = queries.shape[1] // head_dim
    heads_per_target = query_heads // groups
    page_size = slot_tokens * groups
    pages = page_slot_table.shape[1]

    both = jnp.concatenate(
        [key_value_weight, adapter_down_weight.reshape(adapter_down_weight.shape[0], -1)], axis=1
    )
    products = jnp.dot(normed_token_input, both, preferred_element_type=jnp.float32)
    base_part = products[:, :column_span]
    down_all = products[:, column_span:].reshape(request_count, local_adapters, rank_width)
    local_choice = selected_adapter - group_index * local_adapters
    picker = (local_choice[:, None] == jnp.arange(local_adapters, dtype=jnp.int32)[None, :]).astype(
        jnp.float32
    )
    mid_part = jnp.einsum("ia,iaw->iw", picker, down_all)
    partial = jnp.concatenate([base_part, mid_part], axis=1).reshape(homes, rows, -1)
    summed = jnp.sum(lax.all_to_all(partial, "req", 0, 0, tiled=False), axis=0)
    base_resident = summed[:, :column_span]
    mid_owned = summed[:, column_span:].astype(jnp.bfloat16)

    resident_adapters = lax.dynamic_slice_in_dim(selected_adapter, home_index * rows, rows)
    owner = resident_adapters // local_adapters
    mid_spread = lax.all_to_all(
        jnp.broadcast_to(mid_owned[None], (groups,) + mid_owned.shape), "grp", 0, 0, tiled=False
    )
    request_index = jnp.arange(rows, dtype=jnp.int32)
    mid_home = mid_spread[owner, request_index]
    is_value = group_index * column_span >= key_width
    mid_used = jnp.where(is_value, mid_home[:, rank_half:], mid_home[:, :rank_half])
    up_weight_rows = adapter_up_weight[resident_adapters]
    adapter_update = jnp.einsum(
        "ir,irc->ic", mid_used, up_weight_rows, preferred_element_type=jnp.float32
    )
    fresh_columns = (base_resident + adapter_scale * adapter_update).astype(jnp.bfloat16)

    gathered = key_value_pages[page_slot_table][:, :, 0]
    keys = gathered[:, :, 0]
    values = gathered[:, :, 1]
    query = queries.reshape(rows, heads, -1, head_dim)
    scores = jnp.einsum(
        "ihgd,inhd->ihgn", query, keys, preferred_element_type=jnp.float32
    ) / math.sqrt(head_dim)
    positions = jnp.arange(pages, dtype=jnp.int32) * page_size + group_index * slot_tokens
    valid = (positions[None, :] < lengths[:, None])[:, None, None, :]
    scores = jnp.where(valid, scores, masked_score)
    local_top = jnp.max(scores, axis=3)
    weights = jnp.where(valid, jnp.exp(scores - local_top[..., None]), 0.0)
    local_total = jnp.sum(weights, axis=3)
    local_mixed = jnp.einsum(
        "ihgn,inhd->ihgd", weights, values, preferred_element_type=jnp.float32
    )

    parcel = jnp.concatenate(
        [
            local_mixed.reshape(rows, groups, heads_per_target * head_dim),
            local_top.reshape(rows, groups, heads_per_target),
            local_total.reshape(rows, groups, heads_per_target),
            jnp.broadcast_to(
                fresh_columns.astype(jnp.float32)[:, None, :], (rows, groups, column_span)
            ),
        ],
        axis=2,
    ).transpose(1, 0, 2)
    received = lax.all_to_all(parcel, "grp", 0, 0, tiled=False)
    mixed_width = heads_per_target * head_dim
    shard_mixed = received[:, :, :mixed_width].reshape(groups, rows, heads_per_target, head_dim)
    shard_top = received[:, :, mixed_width : mixed_width + heads_per_target]
    shard_total = received[:, :, mixed_width + heads_per_target : mixed_width + 2 * heads_per_target]
    new_all = received[:, :, mixed_width + 2 * heads_per_target :].astype(jnp.bfloat16)
    new_all = new_all.transpose(1, 0, 2).reshape(rows, groups * column_span)
    new_keys = new_all[:, :key_width].reshape(rows, heads, head_dim)
    new_values = new_all[:, key_width:].reshape(rows, heads, head_dim)

    head_of_target = group_index * heads_per_target // (query_heads // heads)
    own_query = lax.dynamic_slice_in_dim(
        queries, group_index * mixed_width, mixed_width, axis=1
    ).reshape(rows, heads_per_target, head_dim)
    own_key = lax.dynamic_index_in_dim(new_keys, head_of_target, 1, False)
    own_value = lax.dynamic_index_in_dim(new_values, head_of_target, 1, False)
    new_score = jnp.einsum(
        "ihd,id->ih", own_query, own_key, preferred_element_type=jnp.float32
    ) / math.sqrt(head_dim)
    top = jnp.maximum(jnp.max(shard_top, axis=0), new_score)
    shard_scale = jnp.exp(shard_top - top[None])
    new_weight = jnp.exp(new_score - top)
    total = jnp.sum(shard_total * shard_scale, axis=0) + new_weight
    mixed = jnp.sum(shard_mixed * shard_scale[..., None], axis=0) + new_weight[
        ..., None
    ] * own_value.astype(jnp.float32)[:, None, :]
    own_attention = (mixed / total[..., None]).astype(jnp.bfloat16).reshape(rows, mixed_width)
    attention = lax.all_gather(own_attention, "grp", axis=1, tiled=True)

    page_slot = page_slot_table[request_index, lengths // page_size]
    offset = lengths % page_size
    mine = offset // slot_tokens == group_index
    token_local = offset % slot_tokens
    current = key_value_pages[page_slot, token_local]
    fresh = jnp.stack([new_keys, new_values], axis=1)
    written = key_value_pages.at[page_slot, token_local].set(
        jnp.where(mine[:, None, None, None], fresh, current)
    )

    targets = departing_target[:, 0]
    count_out = departing_slots.shape[0]
    order = jnp.arange(count_out, dtype=jnp.int32)
    earlier = (targets[:, None] == targets[None, :]) & (order[None, :] < order[:, None])
    place = jnp.sum(earlier.astype(jnp.int32), axis=1)
    live_slots = rows * pages
    capacity = (key_value_pages.shape[0] - live_slots) // homes
    outbound = (
        jnp.zeros((homes, capacity) + key_value_pages.shape[1:], key_value_pages.dtype)
        .at[targets, place]
        .set(written[departing_slots])
    )
    arrived = lax.all_to_all(outbound, "req", split_axis=0, concat_axis=0, tiled=True)
    migrated_pool = jnp.concatenate(
        [
            written[:live_slots],
            arrived.reshape((homes * capacity,) + key_value_pages.shape[1:]),
        ],
        axis=0,
    )
    return (attention, migrated_pool)


def solution(mesh):
    in_specs = (
        P(None, "req"),
        P("req", "grp"),
        P("req", "grp", None),
        P(None, None, "grp"),
        P(),
        P("req", None),
        P("req", "grp", None, None, None),
        P("req"),
        P("req", None),
        P("req"),
        P("req", None),
    )
    out_specs = (P("req", None), P("req", "grp", None, None, None))
    return jax.shard_map(shards, mesh=mesh, in_specs=in_specs, out_specs=out_specs, check_vma=False)
```

```python
import math

import jax
import jax.numpy as jnp
from jax import lax
from jax.sharding import PartitionSpec as P

adapter_scale = 2.0
masked_score = -1e30


def shards(
    normed_token_input,
    key_value_weight,
    adapter_down_weight,
    adapter_up_weight,
    adapter_index_rows,
    queries,
    key_value_pages,
    lengths,
    page_slot_table,
    departing_slots,
    departing_target,
):
    selected_adapter = adapter_index_rows[:, 0]
    homes = lax.axis_size("req")
    groups = lax.axis_size("grp")
    home_index = lax.axis_index("req")
    group_index = lax.axis_index("grp")
    rows = lengths.shape[0]
    request_count = normed_token_input.shape[0]
    column_span = key_value_weight.shape[1]
    local_adapters = adapter_down_weight.shape[1]
    rank_width = adapter_down_weight.shape[2]
    rank_half = adapter_up_weight.shape[1]
    slot_tokens = key_value_pages.shape[1]
    heads = key_value_pages.shape[3]
    head_dim = key_value_pages.shape[4]
    key_width = heads * head_dim
    query_heads = queries.shape[1] // head_dim
    heads_per_target = query_heads // groups
    page_size = slot_tokens * groups
    pages = page_slot_table.shape[1]

    both = jnp.concatenate(
        [key_value_weight, adapter_down_weight.reshape(adapter_down_weight.shape[0], -1)], axis=1
    )
    products = jnp.dot(normed_token_input, both, preferred_element_type=jnp.float32)
    base_part = products[:, :column_span]
    down_all = products[:, column_span:].reshape(request_count, local_adapters, rank_width)
    local_choice = selected_adapter - group_index * local_adapters
    picker = (local_choice[:, None] == jnp.arange(local_adapters, dtype=jnp.int32)[None, :]).astype(
        jnp.float32
    )
    mid_part = jnp.einsum("ia,iaw->iw", picker, down_all)
    partial = jnp.concatenate([base_part, mid_part], axis=1).reshape(homes, rows, -1)
    summed = jnp.sum(lax.all_to_all(partial, "req", 0, 0, tiled=False), axis=0)
    base_resident = summed[:, :column_span]
    mid_owned = summed[:, column_span:].astype(jnp.bfloat16)

    resident_adapters = lax.dynamic_slice_in_dim(selected_adapter, home_index * rows, rows)
    owner = resident_adapters // local_adapters
    mid_spread = lax.all_to_all(
        jnp.broadcast_to(mid_owned[None], (groups,) + mid_owned.shape), "grp", 0, 0, tiled=False
    )
    request_index = jnp.arange(rows, dtype=jnp.int32)
    mid_home = mid_spread[owner, request_index]
    is_value = group_index * column_span >= key_width
    mid_used = jnp.where(is_value, mid_home[:, rank_half:], mid_home[:, :rank_half])
    up_weight_rows = adapter_up_weight[resident_adapters]
    adapter_update = jnp.einsum(
        "ir,irc->ic", mid_used, up_weight_rows, preferred_element_type=jnp.float32
    )
    fresh_columns = (base_resident + adapter_scale * adapter_update).astype(jnp.bfloat16)

    gathered = key_value_pages[page_slot_table][:, :, 0]
    keys = gathered[:, :, 0]
    values = gathered[:, :, 1]
    query = queries.reshape(rows, heads, -1, head_dim)
    scores = jnp.einsum(
        "ihgd,inhd->ihgn", query, keys, preferred_element_type=jnp.float32
    ) / math.sqrt(head_dim)
    positions = jnp.arange(pages, dtype=jnp.int32) * page_size + group_index * slot_tokens
    valid = (positions[None, :] < lengths[:, None])[:, None, None, :]
    scores = jnp.where(valid, scores, masked_score)
    local_top = jnp.max(scores, axis=3)
    weights = jnp.where(valid, jnp.exp(scores - local_top[..., None]), 0.0)
    local_total = jnp.sum(weights, axis=3)
    local_mixed = jnp.einsum(
        "ihgn,inhd->ihgd", weights, values, preferred_element_type=jnp.float32
    )

    parcel = jnp.concatenate(
        [
            local_mixed.reshape(rows, groups, heads_per_target * head_dim),
            local_top.reshape(rows, groups, heads_per_target),
            local_total.reshape(rows, groups, heads_per_target),
            jnp.broadcast_to(
                fresh_columns.astype(jnp.float32)[:, None, :], (rows, groups, column_span)
            ),
        ],
        axis=2,
    ).transpose(1, 0, 2)
    received = lax.all_to_all(parcel, "grp", 0, 0, tiled=False)
    mixed_width = heads_per_target * head_dim
    shard_mixed = received[:, :, :mixed_width].reshape(groups, rows, heads_per_target, head_dim)
    shard_top = received[:, :, mixed_width : mixed_width + heads_per_target]
    shard_total = received[:, :, mixed_width + heads_per_target : mixed_width + 2 * heads_per_target]
    new_all = received[:, :, mixed_width + 2 * heads_per_target :].astype(jnp.bfloat16)
    new_all = new_all.transpose(1, 0, 2).reshape(rows, groups * column_span)
    new_keys = new_all[:, :key_width].reshape(rows, heads, head_dim)
    new_values = new_all[:, key_width:].reshape(rows, heads, head_dim)

    head_of_target = group_index * heads_per_target // (query_heads // heads)
    own_query = lax.dynamic_slice_in_dim(
        queries, group_index * mixed_width, mixed_width, axis=1
    ).reshape(rows, heads_per_target, head_dim)
    own_key = lax.dynamic_index_in_dim(new_keys, head_of_target, 1, False)
    own_value = lax.dynamic_index_in_dim(new_values, head_of_target, 1, False)
    new_score = jnp.einsum(
        "ihd,id->ih", own_query, own_key, preferred_element_type=jnp.float32
    ) / math.sqrt(head_dim)
    top = jnp.maximum(jnp.max(shard_top, axis=0), new_score)
    shard_scale = jnp.exp(shard_top - top[None])
    new_weight = jnp.exp(new_score - top)
    total = jnp.sum(shard_total * shard_scale, axis=0) + new_weight
    mixed = jnp.sum(shard_mixed * shard_scale[..., None], axis=0) + new_weight[
        ..., None
    ] * own_value.astype(jnp.float32)[:, None, :]
    own_attention = (mixed / total[..., None]).astype(jnp.bfloat16).reshape(rows, mixed_width)
    attention = lax.all_to_all(
        jnp.broadcast_to(own_attention[None], (groups,) + own_attention.shape), "grp", 0, 0, tiled=False
    )
    attention = attention.transpose(1, 0, 2).reshape(rows, groups * mixed_width)

    page_slot = page_slot_table[request_index, lengths // page_size]
    offset = lengths % page_size
    mine = offset // slot_tokens == group_index
    token_local = offset % slot_tokens
    current = key_value_pages[page_slot, token_local]
    fresh = jnp.stack([new_keys, new_values], axis=1)
    written = key_value_pages.at[page_slot, token_local].set(
        jnp.where(mine[:, None, None, None], fresh, current)
    )

    targets = departing_target[:, 0]
    count_out = departing_slots.shape[0]
    order = jnp.arange(count_out, dtype=jnp.int32)
    earlier = (targets[:, None] == targets[None, :]) & (order[None, :] < order[:, None])
    place = jnp.sum(earlier.astype(jnp.int32), axis=1)
    live_slots = rows * pages
    capacity = (key_value_pages.shape[0] - live_slots) // homes
    outbound = (
        jnp.zeros((homes, capacity) + key_value_pages.shape[1:], key_value_pages.dtype)
        .at[targets, place]
        .set(written[departing_slots])
    )
    arrived = lax.all_to_all(outbound, "req", split_axis=0, concat_axis=0, tiled=True)
    migrated_pool = jnp.concatenate(
        [
            written[:live_slots],
            arrived.reshape((homes * capacity,) + key_value_pages.shape[1:]),
        ],
        axis=0,
    )
    return (attention, migrated_pool)


def solution(mesh):
    in_specs = (
        P(None, "req"),
        P("req", "grp"),
        P("req", "grp", None),
        P(None, None, "grp"),
        P(),
        P("req", None),
        P("req", "grp", None, None, None),
        P("req"),
        P("req", None),
        P("req"),
        P("req", None),
    )
    out_specs = (P("req", None), P("req", "grp", None, None, None))
    return jax.shard_map(shards, mesh=mesh, in_specs=in_specs, out_specs=out_specs, check_vma=False)
```

```python
import math

import jax
import jax.numpy as jnp
from jax import lax
from jax.sharding import PartitionSpec as P

adapter_scale = 2.0
masked_score = -1e30


def shards(
    normed_token_input,
    key_value_weight,
    adapter_down_weight,
    adapter_up_weight,
    adapter_index_rows,
    queries,
    key_value_pages,
    lengths,
    page_slot_table,
    departing_slots,
    departing_target,
):
    selected_adapter = adapter_index_rows[:, 0]
    homes = lax.axis_size("req")
    groups = lax.axis_size("grp")
    home_index = lax.axis_index("req")
    group_index = lax.axis_index("grp")
    rows = lengths.shape[0]
    request_count = normed_token_input.shape[0]
    column_span = key_value_weight.shape[1]
    local_adapters = adapter_down_weight.shape[1]
    rank_width = adapter_down_weight.shape[2]
    rank_half = adapter_up_weight.shape[1]
    slot_tokens = key_value_pages.shape[1]
    heads = key_value_pages.shape[3]
    head_dim = key_value_pages.shape[4]
    key_width = heads * head_dim
    query_heads = queries.shape[1] // head_dim
    heads_per_target = query_heads // groups
    page_size = slot_tokens * groups
    pages = page_slot_table.shape[1]

    both = jnp.concatenate(
        [key_value_weight, adapter_down_weight.reshape(adapter_down_weight.shape[0], -1)], axis=1
    )
    by_home = normed_token_input.reshape(homes, rows, -1)
    products = jnp.einsum("hiw,wc->hic", by_home, both, preferred_element_type=jnp.float32)
    base_part = products[:, :, :column_span]
    down_all = products[:, :, column_span:].reshape(homes, rows, local_adapters, rank_width)
    local_choice = (selected_adapter - group_index * local_adapters).reshape(homes, rows)
    picker = (
        local_choice[:, :, None] == jnp.arange(local_adapters, dtype=jnp.int32)[None, None, :]
    ).astype(jnp.float32)
    mid_part = jnp.einsum("hia,hiaw->hiw", picker, down_all)
    partial = jnp.concatenate([base_part, mid_part], axis=2)
    resident_adapters = lax.dynamic_slice_in_dim(selected_adapter, home_index * rows, rows)
    up_weight_rows = adapter_up_weight[resident_adapters]
    summed, up_weight_rows = lax.optimization_barrier(
        (lax.all_to_all(partial, "req", 0, 0, tiled=False), up_weight_rows)
    )
    summed = jnp.sum(summed, axis=0)
    base_resident = summed[:, :column_span]
    mid_owned = summed[:, column_span:].astype(jnp.bfloat16)

    owner = resident_adapters // local_adapters
    mid_spread = lax.all_to_all(
        jnp.broadcast_to(mid_owned[None], (groups,) + mid_owned.shape), "grp", 0, 0, tiled=False
    )
    request_index = jnp.arange(rows, dtype=jnp.int32)
    mid_home = mid_spread[owner, request_index]
    is_value = group_index * column_span >= key_width
    mid_used = jnp.where(is_value, mid_home[:, rank_half:], mid_home[:, :rank_half])
    adapter_update = jnp.einsum(
        "ir,irc->ic", mid_used, up_weight_rows, preferred_element_type=jnp.float32
    )
    fresh_columns = (base_resident + adapter_scale * adapter_update).astype(jnp.bfloat16)

    gathered = key_value_pages[page_slot_table][:, :, 0]
    keys = gathered[:, :, 0]
    values = gathered[:, :, 1]
    query = queries.reshape(rows, heads, -1, head_dim)
    scores = jnp.einsum(
        "ihgd,inhd->ihgn", query, keys, preferred_element_type=jnp.float32
    ) / math.sqrt(head_dim)
    positions = jnp.arange(pages, dtype=jnp.int32) * page_size + group_index * slot_tokens
    valid = (positions[None, :] < lengths[:, None])[:, None, None, :]
    scores = jnp.where(valid, scores, masked_score)
    local_top = jnp.max(scores, axis=3)
    weights = jnp.where(valid, jnp.exp(scores - local_top[..., None]), 0.0)
    local_total = jnp.sum(weights, axis=3)
    local_mixed = jnp.einsum(
        "ihgn,inhd->ihgd", weights, values, preferred_element_type=jnp.float32
    )

    parcel = jnp.concatenate(
        [
            local_mixed.reshape(rows, groups, heads_per_target * head_dim),
            local_top.reshape(rows, groups, heads_per_target),
            local_total.reshape(rows, groups, heads_per_target),
            jnp.broadcast_to(
                fresh_columns.astype(jnp.float32)[:, None, :], (rows, groups, column_span)
            ),
        ],
        axis=2,
    ).transpose(1, 0, 2)
    received = lax.all_to_all(parcel, "grp", 0, 0, tiled=False)
    mixed_width = heads_per_target * head_dim
    shard_mixed = received[:, :, :mixed_width].reshape(groups, rows, heads_per_target, head_dim)
    shard_top = received[:, :, mixed_width : mixed_width + heads_per_target]
    shard_total = received[:, :, mixed_width + heads_per_target : mixed_width + 2 * heads_per_target]
    new_all = received[:, :, mixed_width + 2 * heads_per_target :].astype(jnp.bfloat16)
    new_all = new_all.transpose(1, 0, 2).reshape(rows, groups * column_span)
    new_keys = new_all[:, :key_width].reshape(rows, heads, head_dim)
    new_values = new_all[:, key_width:].reshape(rows, heads, head_dim)

    head_of_target = group_index * heads_per_target // (query_heads // heads)
    own_query = lax.dynamic_slice_in_dim(
        queries, group_index * mixed_width, mixed_width, axis=1
    ).reshape(rows, heads_per_target, head_dim)
    own_key = lax.dynamic_index_in_dim(new_keys, head_of_target, 1, False)
    own_value = lax.dynamic_index_in_dim(new_values, head_of_target, 1, False)
    new_score = jnp.einsum(
        "ihd,id->ih", own_query, own_key, preferred_element_type=jnp.float32
    ) / math.sqrt(head_dim)
    top = jnp.maximum(jnp.max(shard_top, axis=0), new_score)
    shard_scale = jnp.exp(shard_top - top[None])
    new_weight = jnp.exp(new_score - top)
    total = jnp.sum(shard_total * shard_scale, axis=0) + new_weight
    mixed = jnp.sum(shard_mixed * shard_scale[..., None], axis=0) + new_weight[
        ..., None
    ] * own_value.astype(jnp.float32)[:, None, :]
    own_attention = (mixed / total[..., None]).astype(jnp.bfloat16).reshape(rows, mixed_width)
    attention = lax.all_to_all(
        jnp.broadcast_to(own_attention[None], (groups,) + own_attention.shape), "grp", 0, 0, tiled=False
    )
    attention = attention.transpose(1, 0, 2).reshape(rows, groups * mixed_width)

    targets = departing_target[:, 0]
    count_out = departing_slots.shape[0]
    order = jnp.arange(count_out, dtype=jnp.int32)
    earlier = (targets[:, None] == targets[None, :]) & (order[None, :] < order[:, None])
    place = jnp.sum(earlier.astype(jnp.int32), axis=1)
    live_slots = rows * pages
    capacity = (key_value_pages.shape[0] - live_slots) // homes
    lands = (targets[None, None, :] == jnp.arange(homes, dtype=jnp.int32)[:, None, None]) & (
        place[None, None, :] == jnp.arange(capacity, dtype=jnp.int32)[None, :, None]
    )
    filled = jnp.any(lands, axis=2)
    source_slot = jnp.sum(jnp.where(lands, departing_slots[None, None, :], 0), axis=2)

    page_slot = page_slot_table[request_index, lengths // page_size]
    offset = lengths % page_size
    mine = offset // slot_tokens == group_index
    token_local = offset % slot_tokens
    current = key_value_pages[page_slot, token_local]
    fresh = jnp.stack([new_keys, new_values], axis=1)
    written = key_value_pages.at[page_slot, token_local].set(
        jnp.where(mine[:, None, None, None], fresh, current)
    )
    attention, written = lax.optimization_barrier((attention, written))

    outbound = jnp.where(
        filled[:, :, None, None, None, None],
        written[source_slot],
        jnp.zeros((), key_value_pages.dtype),
    )
    arrived = lax.all_to_all(outbound, "req", split_axis=0, concat_axis=0, tiled=True)
    migrated_pool = lax.dynamic_update_slice_in_dim(
        written,
        arrived.reshape((homes * capacity,) + key_value_pages.shape[1:]),
        live_slots,
        axis=0,
    )
    return (attention, migrated_pool)


def solution(mesh):
    in_specs = (
        P(None, "req"),
        P("req", "grp"),
        P("req", "grp", None),
        P(None, None, "grp"),
        P(),
        P("req", None),
        P("req", "grp", None, None, None),
        P("req"),
        P("req", None),
        P("req"),
        P("req", None),
    )
    out_specs = (P("req", None), P("req", "grp", None, None, None))
    return jax.shard_map(shards, mesh=mesh, in_specs=in_specs, out_specs=out_specs, check_vma=False)
```

```python
import math

import jax
import jax.numpy as jnp
from jax import lax
from jax.sharding import PartitionSpec as P

adapter_scale = 2.0
masked_score = -1e30


def shards(
    normed_token_input,
    key_value_weight,
    adapter_down_weight,
    adapter_up_weight,
    adapter_index_rows,
    queries,
    key_value_pages,
    lengths,
    page_slot_table,
    departing_slots,
    departing_target,
):
    selected_adapter = adapter_index_rows[:, 0]
    homes = lax.axis_size("req")
    groups = lax.axis_size("grp")
    home_index = lax.axis_index("req")
    group_index = lax.axis_index("grp")
    rows = lengths.shape[0]
    request_count = normed_token_input.shape[0]
    column_span = key_value_weight.shape[1]
    local_adapters = adapter_down_weight.shape[1]
    rank_width = adapter_down_weight.shape[2]
    rank_half = adapter_up_weight.shape[1]
    slot_tokens = key_value_pages.shape[1]
    heads = key_value_pages.shape[3]
    head_dim = key_value_pages.shape[4]
    key_width = heads * head_dim
    query_heads = queries.shape[1] // head_dim
    heads_per_target = query_heads // groups
    page_size = slot_tokens * groups
    pages = page_slot_table.shape[1]

    both = jnp.concatenate(
        [key_value_weight, adapter_down_weight.reshape(adapter_down_weight.shape[0], -1)], axis=1
    )
    by_home = normed_token_input.reshape(homes, rows, -1)
    products = jnp.einsum("hiw,wc->hic", by_home, both, preferred_element_type=jnp.float32)
    base_part = products[:, :, :column_span]
    down_all = products[:, :, column_span:].reshape(homes, rows, local_adapters, rank_width)
    local_choice = (selected_adapter - group_index * local_adapters).reshape(homes, rows)
    picker = (
        local_choice[:, :, None] == jnp.arange(local_adapters, dtype=jnp.int32)[None, None, :]
    ).astype(jnp.float32)
    mid_part = jnp.einsum("hia,hiaw->hiw", picker, down_all)
    partial = jnp.concatenate([base_part, mid_part], axis=2)
    resident_adapters = lax.dynamic_slice_in_dim(selected_adapter, home_index * rows, rows)
    up_weight_rows = adapter_up_weight[resident_adapters]
    summed, up_weight_rows = lax.optimization_barrier(
        (lax.all_to_all(partial, "req", 0, 0, tiled=False), up_weight_rows)
    )
    summed = jnp.sum(summed, axis=0)
    base_resident = summed[:, :column_span]

    owner = resident_adapters // local_adapters
    request_index = jnp.arange(rows, dtype=jnp.int32)
    is_value = group_index * column_span >= key_width
    mixed_width = heads_per_target * head_dim

    gathered = key_value_pages[page_slot_table][:, :, 0]
    keys = gathered[:, :, 0]
    values = gathered[:, :, 1]
    query = queries.reshape(rows, heads, -1, head_dim)
    scores = jnp.einsum(
        "ihgd,inhd->ihgn", query, keys, preferred_element_type=jnp.float32
    ) / math.sqrt(head_dim)
    positions = jnp.arange(pages, dtype=jnp.int32) * page_size + group_index * slot_tokens
    valid = (positions[None, :] < lengths[:, None])[:, None, None, :]
    scores = jnp.where(valid, scores, masked_score)
    local_top = jnp.max(scores, axis=3)
    weights = jnp.where(valid, jnp.exp(scores - local_top[..., None]), 0.0)
    local_total = jnp.sum(weights, axis=3)
    local_mixed = jnp.einsum(
        "ihgn,inhd->ihgd", weights, values, preferred_element_type=jnp.float32
    )

    parcel = jnp.concatenate(
        [
            local_mixed.reshape(rows, groups, mixed_width),
            local_top.reshape(rows, groups, heads_per_target),
            local_total.reshape(rows, groups, heads_per_target),
            jnp.broadcast_to(
                summed[:, None, column_span:], (rows, groups, summed.shape[1] - column_span)
            ),
        ],
        axis=2,
    ).transpose(1, 0, 2)
    received = lax.all_to_all(parcel, "grp", 0, 0, tiled=False)
    shard_mixed = received[:, :, :mixed_width].reshape(groups, rows, heads_per_target, head_dim)
    shard_top = received[:, :, mixed_width : mixed_width + heads_per_target]
    shard_total = received[:, :, mixed_width + heads_per_target : mixed_width + 2 * heads_per_target]
    mid_spread = received[:, :, mixed_width + 2 * heads_per_target :]
    top_own = jnp.max(shard_top, axis=0)
    shard_scale = jnp.exp(shard_top - top_own[None])
    total_own = jnp.sum(shard_total * shard_scale, axis=0)
    mixed_own = jnp.sum(shard_mixed * shard_scale[..., None], axis=0)

    mid_home = mid_spread[owner, request_index].astype(jnp.bfloat16)
    mid_used = jnp.where(is_value, mid_home[:, rank_half:], mid_home[:, :rank_half])
    adapter_update = jnp.einsum(
        "ir,irc->ic", mid_used, up_weight_rows, preferred_element_type=jnp.float32
    )
    fresh_columns = (base_resident + adapter_scale * adapter_update).astype(jnp.bfloat16)

    merged = jnp.concatenate(
        [
            mixed_own.reshape(rows, mixed_width),
            top_own,
            total_own,
            fresh_columns.astype(jnp.float32),
        ],
        axis=1,
    )
    everything = lax.all_to_all(
        jnp.broadcast_to(merged[None], (groups,) + merged.shape), "grp", 0, 0, tiled=False
    ).transpose(1, 0, 2)
    all_mixed = everything[:, :, :mixed_width].reshape(rows, query_heads, head_dim)
    all_top = everything[:, :, mixed_width : mixed_width + heads_per_target].reshape(rows, query_heads)
    all_total = everything[
        :, :, mixed_width + heads_per_target : mixed_width + 2 * heads_per_target
    ].reshape(rows, query_heads)
    new_all = everything[:, :, mixed_width + 2 * heads_per_target :].astype(jnp.bfloat16)
    new_all = new_all.reshape(rows, groups * column_span)
    new_keys = new_all[:, :key_width].reshape(rows, heads, head_dim)
    new_values = new_all[:, key_width:].reshape(rows, heads, head_dim)

    new_score = (
        jnp.einsum("ihgd,ihd->ihg", query, new_keys, preferred_element_type=jnp.float32)
        / math.sqrt(head_dim)
    ).reshape(rows, query_heads)
    top = jnp.maximum(all_top, new_score)
    old_scale = jnp.exp(all_top - top)
    new_weight = jnp.exp(new_score - top)
    total = all_total * old_scale + new_weight
    new_value_rows = jnp.broadcast_to(
        new_values.astype(jnp.float32)[:, :, None, :], (rows, heads, query_heads // heads, head_dim)
    ).reshape(rows, query_heads, head_dim)
    mixed = all_mixed * old_scale[..., None] + new_weight[..., None] * new_value_rows
    attention = (mixed / total[..., None]).astype(jnp.bfloat16).reshape(rows, -1)

    targets = departing_target[:, 0]
    count_out = departing_slots.shape[0]
    order = jnp.arange(count_out, dtype=jnp.int32)
    earlier = (targets[:, None] == targets[None, :]) & (order[None, :] < order[:, None])
    place = jnp.sum(earlier.astype(jnp.int32), axis=1)
    live_slots = rows * pages
    capacity = (key_value_pages.shape[0] - live_slots) // homes
    lands = (targets[None, None, :] == jnp.arange(homes, dtype=jnp.int32)[:, None, None]) & (
        place[None, None, :] == jnp.arange(capacity, dtype=jnp.int32)[None, :, None]
    )
    filled = jnp.any(lands, axis=2)
    source_slot = jnp.sum(jnp.where(lands, departing_slots[None, None, :], 0), axis=2)

    page_slot = page_slot_table[request_index, lengths // page_size]
    offset = lengths % page_size
    mine = offset // slot_tokens == group_index
    token_local = offset % slot_tokens
    current = key_value_pages[page_slot, token_local]
    fresh = jnp.stack([new_keys, new_values], axis=1)
    written = key_value_pages.at[page_slot, token_local].set(
        jnp.where(mine[:, None, None, None], fresh, current)
    )

    outbound = jnp.where(
        filled[:, :, None, None, None, None],
        written[source_slot],
        jnp.zeros((), key_value_pages.dtype),
    )
    arrived = lax.all_to_all(outbound, "req", split_axis=0, concat_axis=0, tiled=True)
    migrated_pool = lax.dynamic_update_slice_in_dim(
        written,
        arrived.reshape((homes * capacity,) + key_value_pages.shape[1:]),
        live_slots,
        axis=0,
    )
    return (attention, migrated_pool)


def solution(mesh):
    in_specs = (
        P(None, "req"),
        P("req", "grp"),
        P("req", "grp", None),
        P(None, None, "grp"),
        P(),
        P("req", None),
        P("req", "grp", None, None, None),
        P("req"),
        P("req", None),
        P("req"),
        P("req", None),
    )
    out_specs = (P("req", None), P("req", "grp", None, None, None))
    return jax.shard_map(shards, mesh=mesh, in_specs=in_specs, out_specs=out_specs, check_vma=False)
```

```python
import math

import jax
import jax.numpy as jnp
from jax import lax
from jax.sharding import PartitionSpec as P

adapter_scale = 2.0
masked_score = -1e30


def split_three(value):
    first = lax.reduce_precision(value, exponent_bits=8, mantissa_bits=7)
    rest = value - first
    second = lax.reduce_precision(rest, exponent_bits=8, mantissa_bits=7)
    third = rest - second
    return jnp.concatenate([first, second, third], axis=-1).astype(jnp.bfloat16)


def join_three(parts, width):
    wide = parts.astype(jnp.float32)
    return wide[..., :width] + wide[..., width : 2 * width] + wide[..., 2 * width :]


def finish_attention(all_mixed, all_top, all_total, query, new_keys, new_values):
    rows, heads, group_size, head_dim = query.shape
    query_heads = heads * group_size
    new_score = (
        jnp.einsum("ihgd,ihd->ihg", query, new_keys, preferred_element_type=jnp.float32)
        / math.sqrt(head_dim)
    ).reshape(rows, query_heads)
    top = jnp.maximum(all_top, new_score)
    old_scale = jnp.exp(all_top - top)
    new_weight = jnp.exp(new_score - top)
    total = all_total * old_scale + new_weight
    new_value_rows = jnp.broadcast_to(
        new_values.astype(jnp.float32)[:, :, None, :], (rows, heads, query_heads // heads, head_dim)
    ).reshape(rows, query_heads, head_dim)
    mixed = all_mixed * old_scale[..., None] + new_weight[..., None] * new_value_rows
    attention = (mixed / total[..., None]).astype(jnp.bfloat16).reshape(rows, -1)

    return attention


def shards(
    normed_token_input,
    key_value_weight,
    adapter_down_weight,
    adapter_up_weight,
    adapter_index_rows,
    queries,
    key_value_pages,
    lengths,
    page_slot_table,
    departing_slots,
    departing_target,
):
    selected_adapter = adapter_index_rows[:, 0]
    homes = lax.axis_size("req")
    groups = lax.axis_size("grp")
    home_index = lax.axis_index("req")
    group_index = lax.axis_index("grp")
    rows = lengths.shape[0]
    request_count = normed_token_input.shape[0]
    column_span = key_value_weight.shape[1]
    local_adapters = adapter_down_weight.shape[1]
    rank_width = adapter_down_weight.shape[2]
    rank_half = adapter_up_weight.shape[1]
    slot_tokens = key_value_pages.shape[1]
    heads = key_value_pages.shape[3]
    head_dim = key_value_pages.shape[4]
    key_width = heads * head_dim
    query_heads = queries.shape[1] // head_dim
    heads_per_target = query_heads // groups
    page_size = slot_tokens * groups
    pages = page_slot_table.shape[1]

    both = jnp.concatenate(
        [key_value_weight, adapter_down_weight.reshape(adapter_down_weight.shape[0], -1)], axis=1
    )
    by_home = normed_token_input.reshape(homes, rows, -1)
    products = jnp.einsum("hiw,wc->hic", by_home, both, preferred_element_type=jnp.float32)
    base_part = products[:, :, :column_span]
    down_all = products[:, :, column_span:].reshape(homes, rows, local_adapters, rank_width)
    local_choice = (selected_adapter - group_index * local_adapters).reshape(homes, rows)
    picker = (
        local_choice[:, :, None] == jnp.arange(local_adapters, dtype=jnp.int32)[None, None, :]
    ).astype(jnp.float32)
    mid_part = jnp.einsum("hia,hiaw->hiw", picker, down_all)
    partial = jnp.concatenate([base_part, mid_part], axis=2)
    resident_adapters = lax.dynamic_slice_in_dim(selected_adapter, home_index * rows, rows)
    up_weight_rows = adapter_up_weight[resident_adapters]
    summed, up_weight_rows = lax.optimization_barrier(
        (lax.all_to_all(partial, "req", 0, 0, tiled=False), up_weight_rows)
    )
    summed = jnp.sum(summed, axis=0)
    base_resident = summed[:, :column_span]

    owner = resident_adapters // local_adapters
    request_index = jnp.arange(rows, dtype=jnp.int32)
    is_value = group_index * column_span >= key_width
    mixed_width = heads_per_target * head_dim

    gathered = key_value_pages[page_slot_table][:, :, 0]
    keys = gathered[:, :, 0]
    values = gathered[:, :, 1]
    query = queries.reshape(rows, heads, -1, head_dim)
    scores = jnp.einsum(
        "ihgd,inhd->ihgn", query, keys, preferred_element_type=jnp.float32
    ) / math.sqrt(head_dim)
    positions = jnp.arange(pages, dtype=jnp.int32) * page_size + group_index * slot_tokens
    valid = (positions[None, :] < lengths[:, None])[:, None, None, :]
    scores = jnp.where(valid, scores, masked_score)
    local_top = jnp.max(scores, axis=3)
    weights = jnp.where(valid, jnp.exp(scores - local_top[..., None]), 0.0)
    local_total = jnp.sum(weights, axis=3)
    local_mixed = jnp.einsum(
        "ihgn,inhd->ihgd", weights, values, preferred_element_type=jnp.float32
    )

    parcel = jnp.concatenate(
        [
            local_mixed.reshape(rows, groups, mixed_width).astype(jnp.bfloat16),
            split_three(local_top.reshape(rows, groups, heads_per_target)),
            split_three(local_total.reshape(rows, groups, heads_per_target)),
            jnp.broadcast_to(
                summed[:, None, column_span:].astype(jnp.bfloat16),
                (rows, groups, summed.shape[1] - column_span),
            ),
        ],
        axis=2,
    ).transpose(1, 0, 2)
    received = lax.all_to_all(parcel, "grp", 0, 0, tiled=False)
    stat_width = 3 * heads_per_target
    shard_mixed = (
        received[:, :, :mixed_width]
        .astype(jnp.float32)
        .reshape(groups, rows, heads_per_target, head_dim)
    )
    shard_top = join_three(received[:, :, mixed_width : mixed_width + stat_width], heads_per_target)
    shard_total = join_three(
        received[:, :, mixed_width + stat_width : mixed_width + 2 * stat_width], heads_per_target
    )
    mid_spread = received[:, :, mixed_width + 2 * stat_width :]
    top_own = jnp.max(shard_top, axis=0)
    shard_scale = jnp.exp(shard_top - top_own[None])
    total_own = jnp.sum(shard_total * shard_scale, axis=0)
    mixed_own = jnp.sum(shard_mixed * shard_scale[..., None], axis=0)

    mid_home = mid_spread[owner, request_index]
    mid_used = jnp.where(is_value, mid_home[:, rank_half:], mid_home[:, :rank_half])
    adapter_update = jnp.einsum(
        "ir,irc->ic", mid_used, up_weight_rows, preferred_element_type=jnp.float32
    )
    fresh_columns = (base_resident + adapter_scale * adapter_update).astype(jnp.bfloat16)

    merged = jnp.concatenate(
        [
            mixed_own.reshape(rows, mixed_width).astype(jnp.bfloat16),
            split_three(top_own),
            split_three(total_own),
            fresh_columns,
        ],
        axis=1,
    )
    everything = lax.all_to_all(
        jnp.broadcast_to(merged[None], (groups,) + merged.shape), "grp", 0, 0, tiled=False
    ).transpose(1, 0, 2)
    all_mixed = everything[:, :, :mixed_width].astype(jnp.float32).reshape(rows, query_heads, head_dim)
    all_top = join_three(
        everything[:, :, mixed_width : mixed_width + stat_width], heads_per_target
    ).reshape(rows, query_heads)
    all_total = join_three(
        everything[:, :, mixed_width + stat_width : mixed_width + 2 * stat_width], heads_per_target
    ).reshape(rows, query_heads)
    new_all = everything[:, :, mixed_width + 2 * stat_width :].reshape(rows, groups * column_span)
    new_keys = new_all[:, :key_width].reshape(rows, heads, head_dim)
    new_values = new_all[:, key_width:].reshape(rows, heads, head_dim)

    attention_parts = (all_mixed, all_top, all_total, query, new_keys, new_values)

    targets = departing_target[:, 0]
    count_out = departing_slots.shape[0]
    order = jnp.arange(count_out, dtype=jnp.int32)
    earlier = (targets[:, None] == targets[None, :]) & (order[None, :] < order[:, None])
    place = jnp.sum(earlier.astype(jnp.int32), axis=1)
    live_slots = rows * pages
    capacity = (key_value_pages.shape[0] - live_slots) // homes
    lands = (targets[None, None, :] == jnp.arange(homes, dtype=jnp.int32)[:, None, None]) & (
        place[None, None, :] == jnp.arange(capacity, dtype=jnp.int32)[None, :, None]
    )
    filled = jnp.any(lands, axis=2)
    source_slot = jnp.sum(jnp.where(lands, departing_slots[None, None, :], 0), axis=2)

    page_slot = page_slot_table[request_index, lengths // page_size]
    offset = lengths % page_size
    mine = offset // slot_tokens == group_index
    token_local = offset % slot_tokens
    current = key_value_pages[page_slot, token_local]
    fresh = jnp.stack([new_keys, new_values], axis=1)
    written = key_value_pages.at[page_slot, token_local].set(
        jnp.where(mine[:, None, None, None], fresh, current)
    )

    outbound = jnp.where(
        filled[:, :, None, None, None, None],
        written[source_slot],
        jnp.zeros((), key_value_pages.dtype),
    )
    outbound, attention_parts = lax.optimization_barrier((outbound, attention_parts))
    arrived = lax.all_to_all(outbound, "req", split_axis=0, concat_axis=0, tiled=True)
    attention = finish_attention(*attention_parts)
    migrated_pool = lax.dynamic_update_slice_in_dim(
        written,
        arrived.reshape((homes * capacity,) + key_value_pages.shape[1:]),
        live_slots,
        axis=0,
    )
    return (attention, migrated_pool)


def solution(mesh):
    in_specs = (
        P(None, "req"),
        P("req", "grp"),
        P("req", "grp", None),
        P(None, None, "grp"),
        P(),
        P("req", None),
        P("req", "grp", None, None, None),
        P("req"),
        P("req", None),
        P("req"),
        P("req", None),
    )
    out_specs = (P("req", None), P("req", "grp", None, None, None))
    return jax.shard_map(shards, mesh=mesh, in_specs=in_specs, out_specs=out_specs, check_vma=False)
```

```python
import math

import jax
import jax.numpy as jnp
from jax import lax
from jax.sharding import PartitionSpec as P

adapter_scale = 2.0
masked_score = -1e30


def split_three(value):
    first = lax.reduce_precision(value, exponent_bits=8, mantissa_bits=7)
    rest = value - first
    second = lax.reduce_precision(rest, exponent_bits=8, mantissa_bits=7)
    third = rest - second
    return jnp.concatenate([first, second, third], axis=-1).astype(jnp.bfloat16)


def join_three(parts, width):
    wide = parts.astype(jnp.float32)
    return wide[..., :width] + wide[..., width : 2 * width] + wide[..., 2 * width :]


def finish_attention(all_mixed, all_top, all_total, query, new_keys, new_values):
    rows, heads, group_size, head_dim = query.shape
    new_score = jnp.einsum(
        "ihgd,hid->hgi", query, new_keys, preferred_element_type=jnp.float32
    ) / math.sqrt(head_dim)
    top = jnp.maximum(all_top, new_score)
    old_scale = jnp.exp(all_top - top)
    new_weight = jnp.exp(new_score - top)
    total = all_total * old_scale + new_weight
    mixed = (
        all_mixed * old_scale[..., None]
        + new_weight[..., None] * new_values.astype(jnp.float32)[:, None, :, :]
    )
    attention = (mixed / total[..., None]).astype(jnp.bfloat16)
    return attention.transpose(2, 0, 1, 3).reshape(rows, -1)

def shards(
    normed_token_input,
    key_value_weight,
    adapter_down_weight,
    adapter_up_weight,
    adapter_index_rows,
    queries,
    key_value_pages,
    lengths,
    page_slot_table,
    departing_slots,
    departing_target,
):
    selected_adapter = adapter_index_rows[:, 0]
    homes = lax.axis_size("req")
    groups = lax.axis_size("grp")
    home_index = lax.axis_index("req")
    group_index = lax.axis_index("grp")
    rows = lengths.shape[0]
    request_count = normed_token_input.shape[0]
    column_span = key_value_weight.shape[1]
    local_adapters = adapter_down_weight.shape[1]
    rank_width = adapter_down_weight.shape[2]
    rank_half = adapter_up_weight.shape[1]
    slot_tokens = key_value_pages.shape[1]
    heads = key_value_pages.shape[3]
    head_dim = key_value_pages.shape[4]
    key_width = heads * head_dim
    query_heads = queries.shape[1] // head_dim
    heads_per_target = query_heads // groups
    page_size = slot_tokens * groups
    pages = page_slot_table.shape[1]

    both = jnp.concatenate(
        [key_value_weight, adapter_down_weight.reshape(adapter_down_weight.shape[0], -1)], axis=1
    )
    by_home = normed_token_input.reshape(homes, rows, -1)
    products = jnp.einsum("hiw,wc->hic", by_home, both, preferred_element_type=jnp.float32)
    base_part = products[:, :, :column_span]
    down_all = products[:, :, column_span:].reshape(homes, rows, local_adapters, rank_width)
    local_choice = (selected_adapter - group_index * local_adapters).reshape(homes, rows)
    picker = (
        local_choice[:, :, None] == jnp.arange(local_adapters, dtype=jnp.int32)[None, None, :]
    ).astype(jnp.float32)
    mid_part = jnp.einsum("hia,hiaw->hiw", picker, down_all)
    partial = jnp.concatenate([base_part, mid_part], axis=2)
    resident_adapters = lax.dynamic_slice_in_dim(selected_adapter, home_index * rows, rows)
    up_weight_rows = adapter_up_weight[resident_adapters]
    summed, up_weight_rows = lax.optimization_barrier(
        (lax.all_to_all(partial, "req", 0, 0, tiled=False), up_weight_rows)
    )
    summed = jnp.sum(summed, axis=0)
    base_resident = summed[:, :column_span]

    owner = resident_adapters // local_adapters
    request_index = jnp.arange(rows, dtype=jnp.int32)
    is_value = group_index * column_span >= key_width

    gathered = key_value_pages[page_slot_table][:, :, 0]
    keys = gathered[:, :, 0]
    values = gathered[:, :, 1]
    query = queries.reshape(rows, heads, -1, head_dim)
    group_size = query.shape[2]
    scores = jnp.einsum(
        "ihgd,inhd->hgin", query, keys, preferred_element_type=jnp.float32
    ) / math.sqrt(head_dim)
    positions = jnp.arange(pages, dtype=jnp.int32) * page_size + group_index * slot_tokens
    valid = (positions[None, :] < lengths[:, None])[None, None]
    scores = jnp.where(valid, scores, masked_score)
    local_top = jnp.max(scores, axis=3)
    weights = jnp.where(valid, jnp.exp(scores - local_top[..., None]), 0.0)
    local_total = jnp.sum(weights, axis=3)
    local_mixed = jnp.einsum(
        "hgin,inhd->hgid", weights, values, preferred_element_type=jnp.float32
    )

    block = heads_per_target * rows * head_dim
    stat_count = heads_per_target * rows
    stats = jnp.concatenate(
        [local_top.reshape(groups, stat_count), local_total.reshape(groups, stat_count)], axis=1
    )
    mid_flat = summed[:, column_span:].astype(jnp.bfloat16).reshape(1, -1)
    parcel = jnp.concatenate(
        [
            local_mixed.reshape(groups, block).astype(jnp.bfloat16),
            split_three(stats),
            jnp.broadcast_to(mid_flat, (groups, mid_flat.shape[1])),
        ],
        axis=1,
    )
    received = lax.all_to_all(parcel, "grp", 0, 0, tiled=False)
    stat_end = block + 6 * stat_count
    shard_mixed = received[:, :block].astype(jnp.float32).reshape(
        groups, heads_per_target, rows, head_dim
    )
    shard_stats = join_three(received[:, block:stat_end], 2 * stat_count)
    shard_top = shard_stats[:, :stat_count].reshape(groups, heads_per_target, rows)
    shard_total = shard_stats[:, stat_count:].reshape(groups, heads_per_target, rows)
    mid_spread = received[:, stat_end:].reshape(groups, rows, -1)
    top_own = jnp.max(shard_top, axis=0)
    shard_scale = jnp.exp(shard_top - top_own[None])
    total_own = jnp.sum(shard_total * shard_scale, axis=0)
    mixed_own = jnp.sum(shard_mixed * shard_scale[..., None], axis=0)

    mid_home = mid_spread[owner, request_index]
    mid_used = jnp.where(is_value, mid_home[:, rank_half:], mid_home[:, :rank_half])
    adapter_update = jnp.einsum(
        "ir,irc->ic", mid_used, up_weight_rows, preferred_element_type=jnp.float32
    )
    fresh_columns = (base_resident + adapter_scale * adapter_update).astype(jnp.bfloat16)

    merged = jnp.concatenate(
        [
            mixed_own.reshape(1, block).astype(jnp.bfloat16),
            split_three(
                jnp.concatenate(
                    [top_own.reshape(1, stat_count), total_own.reshape(1, stat_count)], axis=1
                )
            ),
            fresh_columns.reshape(1, -1),
        ],
        axis=1,
    )
    everything = lax.all_to_all(
        jnp.broadcast_to(merged, (groups, merged.shape[1])), "grp", 0, 0, tiled=False
    )
    all_mixed = everything[:, :block].astype(jnp.float32).reshape(heads, group_size, rows, head_dim)
    all_stats = join_three(everything[:, block:stat_end], 2 * stat_count)
    all_top = all_stats[:, :stat_count].reshape(heads, group_size, rows)
    all_total = all_stats[:, stat_count:].reshape(heads, group_size, rows)
    new_all = everything[:, stat_end:].reshape(groups, rows, column_span)
    new_keys = new_all[: groups // 2]
    new_values = new_all[groups // 2 :]
    attention_parts = (all_mixed, all_top, all_total, query, new_keys, new_values)

    targets = departing_target[:, 0]
    count_out = departing_slots.shape[0]
    order = jnp.arange(count_out, dtype=jnp.int32)
    earlier = (targets[:, None] == targets[None, :]) & (order[None, :] < order[:, None])
    place = jnp.sum(earlier.astype(jnp.int32), axis=1)
    live_slots = rows * pages
    capacity = (key_value_pages.shape[0] - live_slots) // homes
    lands = (targets[None, None, :] == jnp.arange(homes, dtype=jnp.int32)[:, None, None]) & (
        place[None, None, :] == jnp.arange(capacity, dtype=jnp.int32)[None, :, None]
    )
    filled = jnp.any(lands, axis=2)
    source_slot = jnp.sum(jnp.where(lands, departing_slots[None, None, :], 0), axis=2)

    page_slot = page_slot_table[request_index, lengths // page_size]
    offset = lengths % page_size
    mine = offset // slot_tokens == group_index
    token_local = offset % slot_tokens
    current = key_value_pages[page_slot, token_local]
    fresh = jnp.stack([new_keys, new_values], axis=0).transpose(2, 0, 1, 3)
    written = key_value_pages.at[page_slot, token_local].set(
        jnp.where(mine[:, None, None, None], fresh, current)
    )

    outbound = jnp.where(
        filled[:, :, None, None, None, None],
        written[source_slot],
        jnp.zeros((), key_value_pages.dtype),
    )
    outbound, attention_parts = lax.optimization_barrier((outbound, attention_parts))
    arrived = lax.all_to_all(outbound, "req", split_axis=0, concat_axis=0, tiled=True)
    attention = finish_attention(*attention_parts)
    migrated_pool = lax.dynamic_update_slice_in_dim(
        written,
        arrived.reshape((homes * capacity,) + key_value_pages.shape[1:]),
        live_slots,
        axis=0,
    )
    return (attention, migrated_pool)


def solution(mesh):
    in_specs = (
        P(None, "req"),
        P("req", "grp"),
        P("req", "grp", None),
        P(None, None, "grp"),
        P(),
        P("req", None),
        P("req", "grp", None, None, None),
        P("req"),
        P("req", None),
        P("req"),
        P("req", None),
    )
    out_specs = (P("req", None), P("req", "grp", None, None, None))
    return jax.shard_map(shards, mesh=mesh, in_specs=in_specs, out_specs=out_specs, check_vma=False)
```

```python
import math

import jax
import jax.numpy as jnp
from jax import lax
from jax.sharding import PartitionSpec as P

adapter_scale = 2.0
masked_score = -1e30


def split_three(value):
    first = lax.reduce_precision(value, exponent_bits=8, mantissa_bits=7)
    rest = value - first
    second = lax.reduce_precision(rest, exponent_bits=8, mantissa_bits=7)
    third = rest - second
    return jnp.concatenate([first, second, third], axis=-1).astype(jnp.bfloat16)


def join_three(parts, width):
    wide = parts.astype(jnp.float32)
    return wide[..., :width] + wide[..., width : 2 * width] + wide[..., 2 * width :]


def finish_attention(all_mixed, all_top, all_total, query, new_keys, new_values):
    rows, heads, group_size, head_dim = query.shape
    new_score = jnp.einsum(
        "ihgd,hid->hgi", query, new_keys, preferred_element_type=jnp.float32
    ) / math.sqrt(head_dim)
    top = jnp.maximum(all_top, new_score)
    old_scale = jnp.exp(all_top - top)
    new_weight = jnp.exp(new_score - top)
    total = all_total * old_scale + new_weight
    mixed = (
        all_mixed * old_scale[..., None]
        + new_weight[..., None] * new_values.astype(jnp.float32)[:, None, :, :]
    )
    attention = (mixed / total[..., None]).astype(jnp.bfloat16)
    return attention.transpose(2, 0, 1, 3).reshape(rows, -1)

def shards(
    normed_token_input,
    key_value_weight,
    adapter_down_weight,
    adapter_up_weight,
    adapter_index_rows,
    queries,
    key_value_pages,
    lengths,
    page_slot_table,
    departing_slots,
    departing_target,
):
    selected_adapter = adapter_index_rows[:, 0]
    homes = lax.axis_size("req")
    groups = lax.axis_size("grp")
    home_index = lax.axis_index("req")
    group_index = lax.axis_index("grp")
    rows = lengths.shape[0]
    request_count = normed_token_input.shape[0]
    column_span = key_value_weight.shape[1]
    local_adapters = adapter_down_weight.shape[1]
    rank_width = adapter_down_weight.shape[2]
    rank_half = adapter_up_weight.shape[1]
    slot_tokens = key_value_pages.shape[1]
    heads = key_value_pages.shape[3]
    head_dim = key_value_pages.shape[4]
    key_width = heads * head_dim
    query_heads = queries.shape[1] // head_dim
    heads_per_target = query_heads // groups
    page_size = slot_tokens * groups
    pages = page_slot_table.shape[1]

    both = jnp.concatenate(
        [key_value_weight, adapter_down_weight.reshape(adapter_down_weight.shape[0], -1)], axis=1
    )
    by_home = normed_token_input.reshape(homes, rows, -1)
    products = jnp.einsum("hiw,wc->hic", by_home, both, preferred_element_type=jnp.float32)
    base_part = products[:, :, :column_span]
    down_all = products[:, :, column_span:].reshape(homes, rows, local_adapters, rank_width)
    local_choice = (selected_adapter - group_index * local_adapters).reshape(homes, rows)
    picker = (
        local_choice[:, :, None] == jnp.arange(local_adapters, dtype=jnp.int32)[None, None, :]
    ).astype(jnp.float32)
    mid_part = jnp.einsum("hia,hiaw->hiw", picker, down_all)
    partial = jnp.concatenate([base_part, mid_part], axis=2)
    resident_adapters = lax.dynamic_slice_in_dim(selected_adapter, home_index * rows, rows)
    up_weight_rows = adapter_up_weight[resident_adapters]
    summed, up_weight_rows = lax.optimization_barrier(
        (lax.all_to_all(partial, "req", 0, 0, tiled=False), up_weight_rows)
    )
    summed = jnp.sum(summed, axis=0)
    base_resident = summed[:, :column_span]

    owner = resident_adapters // local_adapters
    request_index = jnp.arange(rows, dtype=jnp.int32)
    is_value = group_index * column_span >= key_width

    gathered = key_value_pages[page_slot_table][:, :, 0]
    keys = gathered[:, :, 0]
    values = gathered[:, :, 1]
    query = queries.reshape(rows, heads, -1, head_dim)
    group_size = query.shape[2]
    scores = jnp.einsum(
        "ihgd,inhd->hgin", query, keys, preferred_element_type=jnp.float32
    ) / math.sqrt(head_dim)
    positions = jnp.arange(pages, dtype=jnp.int32) * page_size + group_index * slot_tokens
    valid = (positions[None, :] < lengths[:, None])[None, None]
    scores = jnp.where(valid, scores, masked_score)
    local_top = jnp.max(scores, axis=3)
    weights = jnp.where(valid, jnp.exp(scores - local_top[..., None]), 0.0)
    local_total = jnp.sum(weights, axis=3)
    local_mixed = jnp.einsum(
        "hgin,inhd->hgid", weights, values, preferred_element_type=jnp.float32
    )

    block_rows = heads_per_target * rows
    stat_count = heads_per_target * rows
    stat_rows = -(-6 * stat_count // head_dim)
    spare_rows = 8 - stat_rows
    stats = jnp.concatenate(
        [local_top.reshape(groups, stat_count), local_total.reshape(groups, stat_count)], axis=1
    )
    stat_pack = jnp.concatenate(
        [split_three(stats), jnp.zeros((groups, stat_rows * head_dim - 6 * stat_count), jnp.bfloat16)],
        axis=1,
    ).reshape(groups, stat_rows, head_dim)
    mid_rows = summed[:, column_span:].astype(jnp.bfloat16)
    parcel = jnp.concatenate(
        [
            local_mixed.reshape(groups, block_rows, head_dim).astype(jnp.bfloat16),
            jnp.broadcast_to(mid_rows[None], (groups,) + mid_rows.shape),
            stat_pack,
            jnp.zeros((groups, spare_rows, head_dim), jnp.bfloat16),
        ],
        axis=1,
    )
    received = lax.all_to_all(parcel, "grp", 0, 0, tiled=False)
    stat_at = block_rows + rows
    shard_mixed = received[:, :block_rows].astype(jnp.float32).reshape(
        groups, heads_per_target, rows, head_dim
    )
    shard_stats = join_three(
        received[:, stat_at : stat_at + stat_rows].reshape(groups, -1)[:, : 6 * stat_count],
        2 * stat_count,
    )
    shard_top = shard_stats[:, :stat_count].reshape(groups, heads_per_target, rows)
    shard_total = shard_stats[:, stat_count:].reshape(groups, heads_per_target, rows)
    mid_spread = received[:, block_rows:stat_at]
    top_own = jnp.max(shard_top, axis=0)
    shard_scale = jnp.exp(shard_top - top_own[None])
    total_own = jnp.sum(shard_total * shard_scale, axis=0)
    mixed_own = jnp.sum(shard_mixed * shard_scale[..., None], axis=0)

    mid_home = mid_spread[owner, request_index]
    mid_used = jnp.where(is_value, mid_home[:, rank_half:], mid_home[:, :rank_half])
    adapter_update = jnp.einsum(
        "ir,irc->ic", mid_used, up_weight_rows, preferred_element_type=jnp.float32
    )
    fresh_columns = (base_resident + adapter_scale * adapter_update).astype(jnp.bfloat16)

    own_stats = jnp.concatenate(
        [top_own.reshape(1, stat_count), total_own.reshape(1, stat_count)], axis=1
    )
    merged = jnp.concatenate(
        [
            mixed_own.reshape(block_rows, head_dim).astype(jnp.bfloat16),
            fresh_columns,
            jnp.concatenate(
                [
                    split_three(own_stats),
                    jnp.zeros((1, stat_rows * head_dim - 6 * stat_count), jnp.bfloat16),
                ],
                axis=1,
            ).reshape(stat_rows, head_dim),
            jnp.zeros((spare_rows, head_dim), jnp.bfloat16),
        ],
        axis=0,
    )
    everything = lax.all_to_all(
        jnp.broadcast_to(merged[None], (groups,) + merged.shape), "grp", 0, 0, tiled=False
    )
    all_mixed = everything[:, :block_rows].astype(jnp.float32).reshape(
        heads, group_size, rows, head_dim
    )
    all_stats = join_three(
        everything[:, stat_at : stat_at + stat_rows].reshape(groups, -1)[:, : 6 * stat_count],
        2 * stat_count,
    )
    all_top = all_stats[:, :stat_count].reshape(heads, group_size, rows)
    all_total = all_stats[:, stat_count:].reshape(heads, group_size, rows)
    new_all = everything[:, block_rows:stat_at]
    new_keys = new_all[: groups // 2]
    new_values = new_all[groups // 2 :]
    attention_parts = (all_mixed, all_top, all_total, query, new_keys, new_values)

    targets = departing_target[:, 0]
    count_out = departing_slots.shape[0]
    order = jnp.arange(count_out, dtype=jnp.int32)
    earlier = (targets[:, None] == targets[None, :]) & (order[None, :] < order[:, None])
    place = jnp.sum(earlier.astype(jnp.int32), axis=1)
    live_slots = rows * pages
    capacity = (key_value_pages.shape[0] - live_slots) // homes
    lands = (targets[None, None, :] == jnp.arange(homes, dtype=jnp.int32)[:, None, None]) & (
        place[None, None, :] == jnp.arange(capacity, dtype=jnp.int32)[None, :, None]
    )
    filled = jnp.any(lands, axis=2)
    source_slot = jnp.sum(jnp.where(lands, departing_slots[None, None, :], 0), axis=2)

    page_slot = page_slot_table[request_index, lengths // page_size]
    offset = lengths % page_size
    mine = offset // slot_tokens == group_index
    token_local = offset % slot_tokens
    current = key_value_pages[page_slot, token_local]
    fresh = jnp.stack([new_keys, new_values], axis=0).transpose(2, 0, 1, 3)
    written = key_value_pages.at[page_slot, token_local].set(
        jnp.where(mine[:, None, None, None], fresh, current)
    )

    outbound = jnp.where(
        filled[:, :, None, None, None, None],
        written[source_slot],
        jnp.zeros((), key_value_pages.dtype),
    )
    outbound, attention_parts = lax.optimization_barrier((outbound, attention_parts))
    arrived = lax.all_to_all(outbound, "req", split_axis=0, concat_axis=0, tiled=True)
    attention = finish_attention(*attention_parts)
    migrated_pool = lax.dynamic_update_slice_in_dim(
        written,
        arrived.reshape((homes * capacity,) + key_value_pages.shape[1:]),
        live_slots,
        axis=0,
    )
    return (attention, migrated_pool)


def solution(mesh):
    in_specs = (
        P(None, "req"),
        P("req", "grp"),
        P("req", "grp", None),
        P(None, None, "grp"),
        P(),
        P("req", None),
        P("req", "grp", None, None, None),
        P("req"),
        P("req", None),
        P("req"),
        P("req", None),
    )
    out_specs = (P("req", None), P("req", "grp", None, None, None))
    return jax.shard_map(shards, mesh=mesh, in_specs=in_specs, out_specs=out_specs, check_vma=False)
```

```python
import math

import jax
import jax.numpy as jnp
from jax import lax
from jax.sharding import PartitionSpec as P

adapter_scale = 2.0
masked_score = -1e30


def split_three(value):
    first = lax.reduce_precision(value, exponent_bits=8, mantissa_bits=7)
    rest = value - first
    second = lax.reduce_precision(rest, exponent_bits=8, mantissa_bits=7)
    third = rest - second
    return jnp.concatenate([first, second, third], axis=-1).astype(jnp.bfloat16)


def join_three(parts, width):
    wide = parts.astype(jnp.float32)
    return wide[..., :width] + wide[..., width : 2 * width] + wide[..., 2 * width :]


def finish_attention(everything, query, new_keys, new_values):
    rows, heads, group_size, head_dim = query.shape
    block_rows = heads * group_size * rows // everything.shape[0]
    stat_count = block_rows
    stat_at = block_rows + rows
    stat_rows = -(-6 * stat_count // head_dim)
    all_mixed = everything[:, :block_rows].astype(jnp.float32).reshape(
        heads, group_size, rows, head_dim
    )
    all_stats = join_three(
        everything[:, stat_at : stat_at + stat_rows].reshape(everything.shape[0], -1)[
            :, : 6 * stat_count
        ],
        2 * stat_count,
    )
    all_top = all_stats[:, :stat_count].reshape(heads, group_size, rows)
    all_total = all_stats[:, stat_count:].reshape(heads, group_size, rows)
    new_score = jnp.einsum(
        "ihgd,hid->hgi", query, new_keys, preferred_element_type=jnp.float32
    ) / math.sqrt(head_dim)
    top = jnp.maximum(all_top, new_score)
    old_scale = jnp.exp(all_top - top)
    new_weight = jnp.exp(new_score - top)
    total = all_total * old_scale + new_weight
    mixed = (
        all_mixed * old_scale[..., None]
        + new_weight[..., None] * new_values.astype(jnp.float32)[:, None, :, :]
    )
    attention = (mixed / total[..., None]).astype(jnp.bfloat16)
    return attention.transpose(2, 0, 1, 3).reshape(rows, -1)

def shards(
    normed_token_input,
    key_value_weight,
    adapter_down_weight,
    adapter_up_weight,
    adapter_index_rows,
    queries,
    key_value_pages,
    lengths,
    page_slot_table,
    departing_slots,
    departing_target,
):
    selected_adapter = adapter_index_rows[:, 0]
    homes = lax.axis_size("req")
    groups = lax.axis_size("grp")
    home_index = lax.axis_index("req")
    group_index = lax.axis_index("grp")
    rows = lengths.shape[0]
    request_count = normed_token_input.shape[0]
    column_span = key_value_weight.shape[1]
    local_adapters = adapter_down_weight.shape[1]
    rank_width = adapter_down_weight.shape[2]
    rank_half = adapter_up_weight.shape[1]
    slot_tokens = key_value_pages.shape[1]
    heads = key_value_pages.shape[3]
    head_dim = key_value_pages.shape[4]
    key_width = heads * head_dim
    query_heads = queries.shape[1] // head_dim
    heads_per_target = query_heads // groups
    page_size = slot_tokens * groups
    pages = page_slot_table.shape[1]

    both = jnp.concatenate(
        [key_value_weight, adapter_down_weight.reshape(adapter_down_weight.shape[0], -1)], axis=1
    )
    by_home = normed_token_input.reshape(homes, rows, -1)
    products = jnp.einsum("hiw,wc->hic", by_home, both, preferred_element_type=jnp.float32)
    base_part = products[:, :, :column_span]
    down_all = products[:, :, column_span:].reshape(homes, rows, local_adapters, rank_width)
    local_choice = (selected_adapter - group_index * local_adapters).reshape(homes, rows)
    picker = (
        local_choice[:, :, None] == jnp.arange(local_adapters, dtype=jnp.int32)[None, None, :]
    ).astype(jnp.float32)
    mid_part = jnp.einsum("hia,hiaw->hiw", picker, down_all)
    partial = jnp.concatenate([base_part, mid_part], axis=2)
    resident_adapters = lax.dynamic_slice_in_dim(selected_adapter, home_index * rows, rows)
    up_weight_rows = adapter_up_weight[resident_adapters]
    summed, up_weight_rows = lax.optimization_barrier(
        (lax.all_to_all(partial, "req", 0, 0, tiled=False), up_weight_rows)
    )
    summed = jnp.sum(summed, axis=0)
    base_resident = summed[:, :column_span]

    owner = resident_adapters // local_adapters
    request_index = jnp.arange(rows, dtype=jnp.int32)
    is_value = group_index * column_span >= key_width

    gathered = key_value_pages[page_slot_table][:, :, 0]
    keys = gathered[:, :, 0]
    values = gathered[:, :, 1]
    query = queries.reshape(rows, heads, -1, head_dim)
    group_size = query.shape[2]
    scores = jnp.einsum(
        "ihgd,inhd->hgin", query, keys, preferred_element_type=jnp.float32
    ) / math.sqrt(head_dim)
    positions = jnp.arange(pages, dtype=jnp.int32) * page_size + group_index * slot_tokens
    valid = (positions[None, :] < lengths[:, None])[None, None]
    scores = jnp.where(valid, scores, masked_score)
    local_top = jnp.max(scores, axis=3)
    weights = jnp.where(valid, jnp.exp(scores - local_top[..., None]), 0.0)
    local_total = jnp.sum(weights, axis=3)
    local_mixed = jnp.einsum(
        "hgin,inhd->hgid", weights, values, preferred_element_type=jnp.float32
    )

    block_rows = heads_per_target * rows
    stat_count = heads_per_target * rows
    stat_rows = -(-6 * stat_count // head_dim)
    spare_rows = 8 - stat_rows
    stats = jnp.concatenate(
        [local_top.reshape(groups, stat_count), local_total.reshape(groups, stat_count)], axis=1
    )
    stat_pack = jnp.concatenate(
        [split_three(stats), jnp.zeros((groups, stat_rows * head_dim - 6 * stat_count), jnp.bfloat16)],
        axis=1,
    ).reshape(groups, stat_rows, head_dim)
    mid_rows = summed[:, column_span:].astype(jnp.bfloat16)
    parcel = jnp.concatenate(
        [
            local_mixed.reshape(groups, block_rows, head_dim).astype(jnp.bfloat16),
            jnp.broadcast_to(mid_rows[None], (groups,) + mid_rows.shape),
            stat_pack,
            jnp.zeros((groups, spare_rows, head_dim), jnp.bfloat16),
        ],
        axis=1,
    )
    received = lax.all_to_all(parcel, "grp", 0, 0, tiled=False)
    stat_at = block_rows + rows
    shard_mixed = received[:, :block_rows].astype(jnp.float32).reshape(
        groups, heads_per_target, rows, head_dim
    )
    shard_stats = join_three(
        received[:, stat_at : stat_at + stat_rows].reshape(groups, -1)[:, : 6 * stat_count],
        2 * stat_count,
    )
    shard_top = shard_stats[:, :stat_count].reshape(groups, heads_per_target, rows)
    shard_total = shard_stats[:, stat_count:].reshape(groups, heads_per_target, rows)
    mid_spread = received[:, block_rows:stat_at]
    top_own = jnp.max(shard_top, axis=0)
    shard_scale = jnp.exp(shard_top - top_own[None])
    total_own = jnp.sum(shard_total * shard_scale, axis=0)
    mixed_own = jnp.sum(shard_mixed * shard_scale[..., None], axis=0)

    mid_home = mid_spread[owner, request_index]
    mid_used = jnp.where(is_value, mid_home[:, rank_half:], mid_home[:, :rank_half])
    adapter_update = jnp.einsum(
        "ir,irc->ic", mid_used, up_weight_rows, preferred_element_type=jnp.float32
    )
    fresh_columns = (base_resident + adapter_scale * adapter_update).astype(jnp.bfloat16)

    own_stats = jnp.concatenate(
        [top_own.reshape(1, stat_count), total_own.reshape(1, stat_count)], axis=1
    )
    merged = jnp.concatenate(
        [
            mixed_own.reshape(block_rows, head_dim).astype(jnp.bfloat16),
            fresh_columns,
            jnp.concatenate(
                [
                    split_three(own_stats),
                    jnp.zeros((1, stat_rows * head_dim - 6 * stat_count), jnp.bfloat16),
                ],
                axis=1,
            ).reshape(stat_rows, head_dim),
            jnp.zeros((spare_rows, head_dim), jnp.bfloat16),
        ],
        axis=0,
    )
    everything = lax.all_to_all(
        jnp.broadcast_to(merged[None], (groups,) + merged.shape), "grp", 0, 0, tiled=False
    )
    new_all = everything[:, block_rows:stat_at]
    new_keys = new_all[: groups // 2]
    new_values = new_all[groups // 2 :]
    attention_parts = (everything, query, new_keys, new_values)

    targets = departing_target[:, 0]
    count_out = departing_slots.shape[0]
    order = jnp.arange(count_out, dtype=jnp.int32)
    earlier = (targets[:, None] == targets[None, :]) & (order[None, :] < order[:, None])
    place = jnp.sum(earlier.astype(jnp.int32), axis=1)
    live_slots = rows * pages
    capacity = (key_value_pages.shape[0] - live_slots) // homes
    lands = (targets[None, None, :] == jnp.arange(homes, dtype=jnp.int32)[:, None, None]) & (
        place[None, None, :] == jnp.arange(capacity, dtype=jnp.int32)[None, :, None]
    )
    filled = jnp.any(lands, axis=2)
    source_slot = jnp.sum(jnp.where(lands, departing_slots[None, None, :], 0), axis=2)

    page_slot = page_slot_table[request_index, lengths // page_size]
    offset = lengths % page_size
    mine = offset // slot_tokens == group_index
    token_local = offset % slot_tokens
    fresh = jnp.stack([new_keys, new_values], axis=0).transpose(2, 0, 1, 3)
    current = key_value_pages[page_slot, token_local]
    written = key_value_pages.at[page_slot, token_local].set(
        jnp.where(mine[:, None, None, None], fresh, current)
    )

    outbound_old = jnp.where(
        filled[:, :, None, None, None, None],
        key_value_pages[source_slot],
        jnp.zeros((), key_value_pages.dtype),
    )
    hits = (source_slot[:, :, None] == page_slot[None, None, :]) & mine[None, None, :]
    hits = hits & filled[:, :, None]
    patch_request = jnp.argmax(hits, axis=2)
    patched = jnp.any(hits, axis=2)[:, :, None] & (
        jnp.arange(slot_tokens, dtype=jnp.int32)[None, None, :] == token_local[patch_request][:, :, None]
    )
    outbound = jnp.where(
        patched[:, :, :, None, None, None],
        fresh[patch_request][:, :, None],
        outbound_old,
    )
    outbound, attention_parts = lax.optimization_barrier((outbound, attention_parts))
    arrived = lax.all_to_all(outbound, "req", split_axis=0, concat_axis=0, tiled=True)
    attention = finish_attention(*attention_parts)
    migrated_pool = lax.dynamic_update_slice_in_dim(
        written,
        arrived.reshape((homes * capacity,) + key_value_pages.shape[1:]),
        live_slots,
        axis=0,
    )
    return (attention, migrated_pool)


def solution(mesh):
    in_specs = (
        P(None, "req"),
        P("req", "grp"),
        P("req", "grp", None),
        P(None, None, "grp"),
        P(),
        P("req", None),
        P("req", "grp", None, None, None),
        P("req"),
        P("req", None),
        P("req"),
        P("req", None),
    )
    out_specs = (P("req", None), P("req", "grp", None, None, None))
    return jax.shard_map(shards, mesh=mesh, in_specs=in_specs, out_specs=out_specs, check_vma=False)
```

```python
import math

import jax
import jax.numpy as jnp
from jax import lax
from jax.sharding import PartitionSpec as P

adapter_scale = 2.0
masked_score = -1e30


def split_three(value):
    first = lax.reduce_precision(value, exponent_bits=8, mantissa_bits=7)
    rest = value - first
    second = lax.reduce_precision(rest, exponent_bits=8, mantissa_bits=7)
    third = rest - second
    return jnp.concatenate([first, second, third], axis=-1).astype(jnp.bfloat16)


def join_three(parts, width):
    wide = parts.astype(jnp.float32)
    return wide[..., :width] + wide[..., width : 2 * width] + wide[..., 2 * width :]


def finish_attention(all_mixed, all_top, all_total, query, new_keys, new_values):
    rows, heads, group_size, head_dim = query.shape
    new_score = jnp.einsum(
        "ihgd,hid->hgi", query, new_keys, preferred_element_type=jnp.float32
    ) / math.sqrt(head_dim)
    top = jnp.maximum(all_top, new_score)
    old_scale = jnp.exp(all_top - top)
    new_weight = jnp.exp(new_score - top)
    total = all_total * old_scale + new_weight
    mixed = (
        all_mixed * old_scale[..., None]
        + new_weight[..., None] * new_values.astype(jnp.float32)[:, None, :, :]
    )
    attention = (mixed / total[..., None]).astype(jnp.bfloat16)
    return attention.transpose(2, 0, 1, 3).reshape(rows, -1)

def shards(
    normed_token_input,
    key_value_weight,
    adapter_down_weight,
    adapter_up_weight,
    adapter_index_rows,
    queries,
    key_value_pages,
    lengths,
    page_slot_table,
    departing_slots,
    departing_target,
):
    selected_adapter = adapter_index_rows[:, 0]
    homes = lax.axis_size("req")
    groups = lax.axis_size("grp")
    home_index = lax.axis_index("req")
    group_index = lax.axis_index("grp")
    rows = lengths.shape[0]
    request_count = normed_token_input.shape[0]
    column_span = key_value_weight.shape[1]
    local_adapters = adapter_down_weight.shape[1]
    rank_width = adapter_down_weight.shape[2]
    rank_half = adapter_up_weight.shape[1]
    slot_tokens = key_value_pages.shape[1]
    heads = key_value_pages.shape[3]
    head_dim = key_value_pages.shape[4]
    key_width = heads * head_dim
    query_heads = queries.shape[1] // head_dim
    heads_per_target = query_heads // groups
    page_size = slot_tokens * groups
    pages = page_slot_table.shape[1]

    both = jnp.concatenate(
        [key_value_weight, adapter_down_weight.reshape(adapter_down_weight.shape[0], -1)], axis=1
    )
    by_home = normed_token_input.reshape(homes, rows, -1)
    products = jnp.einsum("hiw,wc->hic", by_home, both, preferred_element_type=jnp.float32)
    base_part = products[:, :, :column_span]
    down_all = products[:, :, column_span:].reshape(homes, rows, local_adapters, rank_width)
    local_choice = (selected_adapter - group_index * local_adapters).reshape(homes, rows)
    picker = local_choice[:, :, None] == jnp.arange(local_adapters, dtype=jnp.int32)[None, None, :]
    mid_part = jnp.sum(jnp.where(picker[..., None], down_all, 0.0), axis=2)
    partial = jnp.concatenate([base_part, mid_part], axis=2)
    resident_adapters = lax.dynamic_slice_in_dim(selected_adapter, home_index * rows, rows)
    up_weight_rows = adapter_up_weight[resident_adapters]
    summed, up_weight_rows = lax.optimization_barrier(
        (lax.all_to_all(partial, "req", 0, 0, tiled=False), up_weight_rows)
    )
    summed = jnp.sum(summed, axis=0)
    base_resident = summed[:, :column_span]

    owner = resident_adapters // local_adapters
    request_index = jnp.arange(rows, dtype=jnp.int32)
    is_value = group_index * column_span >= key_width

    gathered = key_value_pages[page_slot_table][:, :, 0]
    keys = gathered[:, :, 0]
    values = gathered[:, :, 1]
    query = queries.reshape(rows, heads, -1, head_dim)
    group_size = query.shape[2]
    scores = jnp.einsum(
        "ihgd,inhd->hgin", query, keys, preferred_element_type=jnp.float32
    ) / math.sqrt(head_dim)
    positions = jnp.arange(pages, dtype=jnp.int32) * page_size + group_index * slot_tokens
    valid = (positions[None, :] < lengths[:, None])[None, None]
    scores = jnp.where(valid, scores, masked_score)
    local_top = jnp.max(scores, axis=3)
    weights = jnp.where(valid, jnp.exp(scores - local_top[..., None]), 0.0)
    local_total = jnp.sum(weights, axis=3)
    local_mixed = jnp.einsum(
        "hgin,inhd->hgid", weights, values, preferred_element_type=jnp.float32
    )

    block_rows = heads_per_target * rows
    stat_count = heads_per_target * rows
    stat_rows = -(-6 * stat_count // head_dim)
    spare_rows = 8 - stat_rows
    stats = jnp.concatenate(
        [local_top.reshape(groups, stat_count), local_total.reshape(groups, stat_count)], axis=1
    )
    stat_pack = jnp.concatenate(
        [split_three(stats), jnp.zeros((groups, stat_rows * head_dim - 6 * stat_count), jnp.bfloat16)],
        axis=1,
    ).reshape(groups, stat_rows, head_dim)
    mid_rows = summed[:, column_span:].astype(jnp.bfloat16)
    parcel = jnp.concatenate(
        [
            local_mixed.reshape(groups, block_rows, head_dim).astype(jnp.bfloat16),
            jnp.broadcast_to(mid_rows[None], (groups,) + mid_rows.shape),
            stat_pack,
            jnp.zeros((groups, spare_rows, head_dim), jnp.bfloat16),
        ],
        axis=1,
    )
    received = lax.all_to_all(parcel, "grp", 0, 0, tiled=False)
    stat_at = block_rows + rows
    shard_mixed = received[:, :block_rows].astype(jnp.float32).reshape(
        groups, heads_per_target, rows, head_dim
    )
    shard_stats = join_three(
        received[:, stat_at : stat_at + stat_rows].reshape(groups, -1)[:, : 6 * stat_count],
        2 * stat_count,
    )
    shard_top = shard_stats[:, :stat_count].reshape(groups, heads_per_target, rows)
    shard_total = shard_stats[:, stat_count:].reshape(groups, heads_per_target, rows)
    mid_spread = received[:, block_rows:stat_at]
    top_own = jnp.max(shard_top, axis=0)
    shard_scale = jnp.exp(shard_top - top_own[None])
    total_own = jnp.sum(shard_total * shard_scale, axis=0)
    mixed_own = jnp.sum(shard_mixed * shard_scale[..., None], axis=0)

    mid_home = mid_spread[owner, request_index]
    mid_used = jnp.where(is_value, mid_home[:, rank_half:], mid_home[:, :rank_half])
    adapter_update = jnp.einsum(
        "ir,irc->ic", mid_used, up_weight_rows, preferred_element_type=jnp.float32
    )
    fresh_columns = (base_resident + adapter_scale * adapter_update).astype(jnp.bfloat16)

    own_stats = jnp.concatenate(
        [top_own.reshape(1, stat_count), total_own.reshape(1, stat_count)], axis=1
    )
    merged = jnp.concatenate(
        [
            mixed_own.reshape(block_rows, head_dim).astype(jnp.bfloat16),
            fresh_columns,
            jnp.concatenate(
                [
                    split_three(own_stats),
                    jnp.zeros((1, stat_rows * head_dim - 6 * stat_count), jnp.bfloat16),
                ],
                axis=1,
            ).reshape(stat_rows, head_dim),
            jnp.zeros((spare_rows, head_dim), jnp.bfloat16),
        ],
        axis=0,
    )
    everything = lax.all_to_all(
        jnp.broadcast_to(merged[None], (groups,) + merged.shape), "grp", 0, 0, tiled=False
    )
    all_mixed = everything[:, :block_rows].astype(jnp.float32).reshape(
        heads, group_size, rows, head_dim
    )
    all_stats = join_three(
        everything[:, stat_at : stat_at + stat_rows].reshape(groups, -1)[:, : 6 * stat_count],
        2 * stat_count,
    )
    all_top = all_stats[:, :stat_count].reshape(heads, group_size, rows)
    all_total = all_stats[:, stat_count:].reshape(heads, group_size, rows)
    new_all = everything[:, block_rows:stat_at]
    new_keys = new_all[: groups // 2]
    new_values = new_all[groups // 2 :]
    attention_parts = (all_mixed, all_top, all_total, query, new_keys, new_values)

    targets = departing_target[:, 0]
    count_out = departing_slots.shape[0]
    order = jnp.arange(count_out, dtype=jnp.int32)
    earlier = (targets[:, None] == targets[None, :]) & (order[None, :] < order[:, None])
    place = jnp.sum(earlier.astype(jnp.int32), axis=1)
    live_slots = rows * pages
    capacity = (key_value_pages.shape[0] - live_slots) // homes
    lands = (targets[None, None, :] == jnp.arange(homes, dtype=jnp.int32)[:, None, None]) & (
        place[None, None, :] == jnp.arange(capacity, dtype=jnp.int32)[None, :, None]
    )
    filled = jnp.any(lands, axis=2)
    source_slot = jnp.sum(jnp.where(lands, departing_slots[None, None, :], 0), axis=2)

    page_slot = page_slot_table[request_index, lengths // page_size]
    offset = lengths % page_size
    mine = offset // slot_tokens == group_index
    token_local = offset % slot_tokens
    current = key_value_pages[page_slot, token_local]
    fresh = jnp.stack([new_keys, new_values], axis=0).transpose(2, 0, 1, 3)
    written = key_value_pages.at[page_slot, token_local].set(
        jnp.where(mine[:, None, None, None], fresh, current)
    )

    outbound = jnp.where(
        filled[:, :, None, None, None, None],
        written[source_slot],
        jnp.zeros((), key_value_pages.dtype),
    )
    outbound, attention_parts = lax.optimization_barrier((outbound, attention_parts))
    arrived = lax.all_to_all(outbound, "req", split_axis=0, concat_axis=0, tiled=True)
    attention = finish_attention(*attention_parts)
    migrated_pool = lax.dynamic_update_slice_in_dim(
        written,
        arrived.reshape((homes * capacity,) + key_value_pages.shape[1:]),
        live_slots,
        axis=0,
    )
    return (attention, migrated_pool)


def solution(mesh):
    in_specs = (
        P(None, "req"),
        P("req", "grp"),
        P("req", "grp", None),
        P(None, None, "grp"),
        P(),
        P("req", None),
        P("req", "grp", None, None, None),
        P("req"),
        P("req", None),
        P("req"),
        P("req", None),
    )
    out_specs = (P("req", None), P("req", "grp", None, None, None))
    return jax.shard_map(shards, mesh=mesh, in_specs=in_specs, out_specs=out_specs, check_vma=False)
```

```python
import math

import jax
import jax.numpy as jnp
from jax import lax
from jax.sharding import PartitionSpec as P

adapter_scale = 2.0
masked_score = -1e30


def split_three(value):
    first = lax.reduce_precision(value, exponent_bits=8, mantissa_bits=7)
    rest = value - first
    second = lax.reduce_precision(rest, exponent_bits=8, mantissa_bits=7)
    third = rest - second
    return jnp.concatenate([first, second, third], axis=-1).astype(jnp.bfloat16)


def join_three(parts, width):
    wide = parts.astype(jnp.float32)
    return wide[..., :width] + wide[..., width : 2 * width] + wide[..., 2 * width :]


def finish_attention(all_mixed, all_top, all_total, query, new_keys, new_values):
    rows, heads, group_size, head_dim = query.shape
    new_score = jnp.einsum(
        "ihgd,hid->hgi", query, new_keys, preferred_element_type=jnp.float32
    ) / math.sqrt(head_dim)
    top = jnp.maximum(all_top, new_score)
    old_scale = jnp.exp(all_top - top)
    new_weight = jnp.exp(new_score - top)
    total = all_total * old_scale + new_weight
    mixed = (
        all_mixed * old_scale[..., None]
        + new_weight[..., None] * new_values.astype(jnp.float32)[:, None, :, :]
    )
    attention = (mixed / total[..., None]).astype(jnp.bfloat16)
    return attention.transpose(2, 0, 1, 3).reshape(rows, -1)

def shards(
    normed_token_input,
    key_value_weight,
    adapter_down_weight,
    adapter_up_weight,
    adapter_index_rows,
    queries,
    key_value_pages,
    lengths,
    page_slot_table,
    departing_slots,
    departing_target,
):
    selected_adapter = adapter_index_rows[:, 0]
    request_index = jnp.arange(lengths.shape[0], dtype=jnp.int32)
    homes = lax.axis_size("req")
    groups = lax.axis_size("grp")
    home_index = lax.axis_index("req")
    group_index = lax.axis_index("grp")
    rows = lengths.shape[0]
    request_count = normed_token_input.shape[0]
    column_span = key_value_weight.shape[1]
    local_adapters = adapter_down_weight.shape[1]
    rank_width = adapter_down_weight.shape[2]
    rank_half = adapter_up_weight.shape[1]
    slot_tokens = key_value_pages.shape[1]
    heads = key_value_pages.shape[3]
    head_dim = key_value_pages.shape[4]
    key_width = heads * head_dim
    query_heads = queries.shape[1] // head_dim
    heads_per_target = query_heads // groups
    page_size = slot_tokens * groups
    pages = page_slot_table.shape[1]

    both = jnp.concatenate(
        [key_value_weight, adapter_down_weight.reshape(adapter_down_weight.shape[0], -1)], axis=1
    )
    by_home = normed_token_input.reshape(homes, rows, -1)
    products = jnp.einsum("hiw,wc->hic", by_home, both, preferred_element_type=jnp.float32)
    base_part = products[:, :, :column_span]
    down_all = products[:, :, column_span:].reshape(homes, rows, local_adapters, rank_width)
    local_choice = (selected_adapter - group_index * local_adapters).reshape(homes, rows)
    picker = local_choice[:, :, None] == jnp.arange(local_adapters, dtype=jnp.int32)[None, None, :]
    mid_part = jnp.sum(jnp.where(picker[..., None], down_all, 0.0), axis=2)
    partial = jnp.concatenate([base_part, mid_part], axis=2)
    resident_adapters = lax.dynamic_slice_in_dim(selected_adapter, home_index * rows, rows)
    up_weight_rows = adapter_up_weight[resident_adapters]
    summed = jnp.sum(lax.all_to_all(partial, "req", 0, 0, tiled=False), axis=0)
    base_resident = summed[:, :column_span]

    owner = resident_adapters // local_adapters
    is_value = group_index * column_span >= key_width

    live_slots = rows * pages
    live = key_value_pages[:live_slots, 0]
    keys = live[:, 0]
    values = live[:, 1]
    query = queries.reshape(rows, heads, -1, head_dim)
    group_size = query.shape[2]
    entry_of_slot = jnp.argmax(
        page_slot_table.reshape(1, -1) == jnp.arange(live_slots, dtype=jnp.int32)[:, None], axis=1
    )
    slot_request = entry_of_slot // pages
    slot_position = (entry_of_slot % pages) * page_size + group_index * slot_tokens
    valid = (slot_request[None, :] == request_index[:, None]) & (
        slot_position[None, :] < lengths[:, None]
    )
    valid = valid[None, None]
    scores = jnp.einsum(
        "ihgd,shd->hgis", query, keys, preferred_element_type=jnp.float32
    ) / math.sqrt(head_dim)
    scores = jnp.where(valid, scores, masked_score)
    local_top = jnp.max(scores, axis=3)
    weights = jnp.where(valid, jnp.exp(scores - local_top[..., None]), 0.0)
    local_total = jnp.sum(weights, axis=3)
    local_mixed = jnp.einsum(
        "hgis,shd->hgid", weights, values, preferred_element_type=jnp.float32
    )

    block_rows = heads_per_target * rows
    stat_count = heads_per_target * rows
    stat_rows = -(-6 * stat_count // head_dim)
    spare_rows = 8 - stat_rows
    stats = jnp.concatenate(
        [local_top.reshape(groups, stat_count), local_total.reshape(groups, stat_count)], axis=1
    )
    stat_pack = jnp.concatenate(
        [split_three(stats), jnp.zeros((groups, stat_rows * head_dim - 6 * stat_count), jnp.bfloat16)],
        axis=1,
    ).reshape(groups, stat_rows, head_dim)
    mid_rows = summed[:, column_span:].astype(jnp.bfloat16)
    parcel = jnp.concatenate(
        [
            local_mixed.reshape(groups, block_rows, head_dim).astype(jnp.bfloat16),
            jnp.broadcast_to(mid_rows[None], (groups,) + mid_rows.shape),
            stat_pack,
            jnp.zeros((groups, spare_rows, head_dim), jnp.bfloat16),
        ],
        axis=1,
    )
    received, up_weight_rows = lax.optimization_barrier(
        (lax.all_to_all(parcel, "grp", 0, 0, tiled=False), up_weight_rows)
    )
    stat_at = block_rows + rows
    shard_mixed = received[:, :block_rows].astype(jnp.float32).reshape(
        groups, heads_per_target, rows, head_dim
    )
    shard_stats = join_three(
        received[:, stat_at : stat_at + stat_rows].reshape(groups, -1)[:, : 6 * stat_count],
        2 * stat_count,
    )
    shard_top = shard_stats[:, :stat_count].reshape(groups, heads_per_target, rows)
    shard_total = shard_stats[:, stat_count:].reshape(groups, heads_per_target, rows)
    mid_spread = received[:, block_rows:stat_at]
    top_own = jnp.max(shard_top, axis=0)
    shard_scale = jnp.exp(shard_top - top_own[None])
    total_own = jnp.sum(shard_total * shard_scale, axis=0)
    mixed_own = jnp.sum(shard_mixed * shard_scale[..., None], axis=0)

    mid_home = mid_spread[owner, request_index]
    mid_used = jnp.where(is_value, mid_home[:, rank_half:], mid_home[:, :rank_half])
    adapter_update = jnp.einsum(
        "ir,irc->ic", mid_used, up_weight_rows, preferred_element_type=jnp.float32
    )
    fresh_columns = (base_resident + adapter_scale * adapter_update).astype(jnp.bfloat16)

    own_stats = jnp.concatenate(
        [top_own.reshape(1, stat_count), total_own.reshape(1, stat_count)], axis=1
    )
    merged = jnp.concatenate(
        [
            mixed_own.reshape(block_rows, head_dim).astype(jnp.bfloat16),
            fresh_columns,
            jnp.concatenate(
                [
                    split_three(own_stats),
                    jnp.zeros((1, stat_rows * head_dim - 6 * stat_count), jnp.bfloat16),
                ],
                axis=1,
            ).reshape(stat_rows, head_dim),
            jnp.zeros((spare_rows, head_dim), jnp.bfloat16),
        ],
        axis=0,
    )
    everything = lax.all_to_all(
        jnp.broadcast_to(merged[None], (groups,) + merged.shape), "grp", 0, 0, tiled=False
    )
    all_mixed = everything[:, :block_rows].astype(jnp.float32).reshape(
        heads, group_size, rows, head_dim
    )
    all_stats = join_three(
        everything[:, stat_at : stat_at + stat_rows].reshape(groups, -1)[:, : 6 * stat_count],
        2 * stat_count,
    )
    all_top = all_stats[:, :stat_count].reshape(heads, group_size, rows)
    all_total = all_stats[:, stat_count:].reshape(heads, group_size, rows)
    new_all = everything[:, block_rows:stat_at]
    new_keys = new_all[: groups // 2]
    new_values = new_all[groups // 2 :]
    attention_parts = (all_mixed, all_top, all_total, query, new_keys, new_values)

    targets = departing_target[:, 0]
    count_out = departing_slots.shape[0]
    order = jnp.arange(count_out, dtype=jnp.int32)
    earlier = (targets[:, None] == targets[None, :]) & (order[None, :] < order[:, None])
    place = jnp.sum(earlier.astype(jnp.int32), axis=1)
    live_slots = rows * pages
    capacity = (key_value_pages.shape[0] - live_slots) // homes
    lands = (targets[None, None, :] == jnp.arange(homes, dtype=jnp.int32)[:, None, None]) & (
        place[None, None, :] == jnp.arange(capacity, dtype=jnp.int32)[None, :, None]
    )
    filled = jnp.any(lands, axis=2)
    source_slot = jnp.sum(jnp.where(lands, departing_slots[None, None, :], 0), axis=2)

    page_slot = page_slot_table[request_index, lengths // page_size]
    offset = lengths % page_size
    mine = offset // slot_tokens == group_index
    token_local = offset % slot_tokens
    current = key_value_pages[page_slot, token_local]
    fresh = jnp.stack([new_keys, new_values], axis=0).transpose(2, 0, 1, 3)
    written = key_value_pages.at[page_slot, token_local].set(
        jnp.where(mine[:, None, None, None], fresh, current)
    )

    outbound = jnp.where(
        filled[:, :, None, None, None, None],
        written[source_slot],
        jnp.zeros((), key_value_pages.dtype),
    )
    outbound, attention_parts = lax.optimization_barrier((outbound, attention_parts))
    arrived = lax.all_to_all(outbound, "req", split_axis=0, concat_axis=0, tiled=True)
    attention = finish_attention(*attention_parts)
    migrated_pool = lax.dynamic_update_slice_in_dim(
        written,
        arrived.reshape((homes * capacity,) + key_value_pages.shape[1:]),
        live_slots,
        axis=0,
    )
    return (attention, migrated_pool)


def solution(mesh):
    in_specs = (
        P(None, "req"),
        P("req", "grp"),
        P("req", "grp", None),
        P(None, None, "grp"),
        P(),
        P("req", None),
        P("req", "grp", None, None, None),
        P("req"),
        P("req", None),
        P("req"),
        P("req", None),
    )
    out_specs = (P("req", None), P("req", "grp", None, None, None))
    return jax.shard_map(shards, mesh=mesh, in_specs=in_specs, out_specs=out_specs, check_vma=False)
```

```python
import math

import jax
import jax.numpy as jnp
from jax import lax
from jax.sharding import PartitionSpec as P

adapter_scale = 2.0
masked_score = -1e30


def split_three(value):
    first = lax.reduce_precision(value, exponent_bits=8, mantissa_bits=7)
    rest = value - first
    second = lax.reduce_precision(rest, exponent_bits=8, mantissa_bits=7)
    third = rest - second
    return jnp.concatenate([first, second, third], axis=-1).astype(jnp.bfloat16)


def join_three(parts, width):
    wide = parts.astype(jnp.float32)
    return wide[..., :width] + wide[..., width : 2 * width] + wide[..., 2 * width :]


def finish_attention(all_mixed, all_top, all_total, query, new_keys, new_values):
    rows, heads, group_size, head_dim = query.shape
    new_score = jnp.einsum(
        "ihgd,hid->hgi", query, new_keys, preferred_element_type=jnp.float32
    ) / math.sqrt(head_dim)
    top = jnp.maximum(all_top, new_score)
    old_scale = jnp.exp(all_top - top)
    new_weight = jnp.exp(new_score - top)
    total = all_total * old_scale + new_weight
    mixed = (
        all_mixed * old_scale[..., None]
        + new_weight[..., None] * new_values.astype(jnp.float32)[:, None, :, :]
    )
    attention = (mixed / total[..., None]).astype(jnp.bfloat16)
    return attention.transpose(2, 0, 1, 3).reshape(rows, -1)

def shards(
    normed_token_input,
    key_value_weight,
    adapter_down_weight,
    adapter_up_weight,
    adapter_index_rows,
    queries,
    key_value_pages,
    lengths,
    page_slot_table,
    departing_slots,
    departing_target,
):
    selected_adapter = adapter_index_rows[:, 0]
    request_index = jnp.arange(lengths.shape[0], dtype=jnp.int32)
    homes = lax.axis_size("req")
    groups = lax.axis_size("grp")
    home_index = lax.axis_index("req")
    group_index = lax.axis_index("grp")
    rows = lengths.shape[0]
    request_count = normed_token_input.shape[0]
    column_span = key_value_weight.shape[1]
    local_adapters = adapter_down_weight.shape[1]
    rank_width = adapter_down_weight.shape[2]
    rank_half = adapter_up_weight.shape[1]
    slot_tokens = key_value_pages.shape[1]
    heads = key_value_pages.shape[3]
    head_dim = key_value_pages.shape[4]
    key_width = heads * head_dim
    query_heads = queries.shape[1] // head_dim
    heads_per_target = query_heads // groups
    page_size = slot_tokens * groups
    pages = page_slot_table.shape[1]

    both = jnp.concatenate(
        [key_value_weight, adapter_down_weight.reshape(adapter_down_weight.shape[0], -1)], axis=1
    )
    by_home = normed_token_input.reshape(homes, rows, -1)
    products = jnp.einsum("hiw,wc->hic", by_home, both, preferred_element_type=jnp.float32)
    base_part = products[:, :, :column_span]
    down_all = products[:, :, column_span:].reshape(homes, rows, local_adapters, rank_width)
    local_choice = (selected_adapter - group_index * local_adapters).reshape(homes, rows)
    picker = local_choice[:, :, None] == jnp.arange(local_adapters, dtype=jnp.int32)[None, None, :]
    mid_part = jnp.sum(jnp.where(picker[..., None], down_all, 0.0), axis=2)
    partial = jnp.concatenate([base_part, mid_part], axis=2)
    resident_adapters = lax.dynamic_slice_in_dim(selected_adapter, home_index * rows, rows)
    up_weight_rows = adapter_up_weight[resident_adapters]
    summed = jnp.sum(lax.all_to_all(partial, "req", 0, 0, tiled=False), axis=0)
    base_resident = summed[:, :column_span]

    owner = resident_adapters // local_adapters
    is_value = group_index * column_span >= key_width

    live_slots = rows * pages
    live = key_value_pages[:live_slots, 0]
    keys = live[:, 0]
    values = live[:, 1]
    query = queries.reshape(rows, heads, -1, head_dim)
    group_size = query.shape[2]
    entry_of_slot = jnp.argmax(
        page_slot_table.reshape(1, -1) == jnp.arange(live_slots, dtype=jnp.int32)[:, None], axis=1
    )
    slot_request = entry_of_slot // pages
    slot_position = (entry_of_slot % pages) * page_size + group_index * slot_tokens
    valid = (slot_request[None, :] == request_index[:, None]) & (
        slot_position[None, :] < lengths[:, None]
    )
    valid = valid[None, None]
    scores = jnp.einsum(
        "ihgd,shd->hgis", query, keys, preferred_element_type=jnp.float32
    ) / math.sqrt(head_dim)
    scores = jnp.where(valid, scores, masked_score)
    local_top = jnp.max(scores, axis=3)
    weights = jnp.where(valid, jnp.exp(scores - local_top[..., None]), 0.0)
    local_total = jnp.sum(weights, axis=3)
    local_mixed = jnp.einsum(
        "hgis,shd->hgid", weights, values, preferred_element_type=jnp.float32
    )

    block_rows = heads_per_target * rows
    stat_count = heads_per_target * rows
    stat_rows = -(-6 * stat_count // head_dim)
    spare_rows = 8 - stat_rows
    stats = jnp.concatenate(
        [local_top.reshape(groups, stat_count), local_total.reshape(groups, stat_count)], axis=1
    )
    stat_pack = jnp.concatenate(
        [split_three(stats), jnp.zeros((groups, stat_rows * head_dim - 6 * stat_count), jnp.bfloat16)],
        axis=1,
    ).reshape(groups, stat_rows, head_dim)
    mid_rows = summed[:, column_span:].astype(jnp.bfloat16)
    parcel = jnp.concatenate(
        [
            local_mixed.reshape(groups, block_rows, head_dim).astype(jnp.bfloat16),
            jnp.broadcast_to(mid_rows[None], (groups,) + mid_rows.shape),
            stat_pack,
            jnp.zeros((groups, spare_rows, head_dim), jnp.bfloat16),
        ],
        axis=1,
    )
    received, up_weight_rows = lax.optimization_barrier(
        (lax.all_to_all(parcel, "grp", 0, 0, tiled=False), up_weight_rows)
    )
    stat_at = block_rows + rows
    shard_mixed = received[:, :block_rows].astype(jnp.float32).reshape(
        groups, heads_per_target, rows, head_dim
    )
    shard_stats = join_three(
        received[:, stat_at : stat_at + stat_rows].reshape(groups, -1)[:, : 6 * stat_count],
        2 * stat_count,
    )
    shard_top = shard_stats[:, :stat_count].reshape(groups, heads_per_target, rows)
    shard_total = shard_stats[:, stat_count:].reshape(groups, heads_per_target, rows)
    mid_spread = received[:, block_rows:stat_at]
    top_own = jnp.max(shard_top, axis=0)
    shard_scale = jnp.exp(shard_top - top_own[None])
    total_own = jnp.sum(shard_total * shard_scale, axis=0)
    mixed_own = jnp.sum(shard_mixed * shard_scale[..., None], axis=0)

    mid_home = mid_spread[owner, request_index]
    mid_used = jnp.where(is_value, mid_home[:, rank_half:], mid_home[:, :rank_half])
    adapter_update = jnp.einsum(
        "ir,irc->ic", mid_used, up_weight_rows, preferred_element_type=jnp.float32
    )
    fresh_columns = (base_resident + adapter_scale * adapter_update).astype(jnp.bfloat16)

    own_stats = jnp.concatenate(
        [top_own.reshape(1, stat_count), total_own.reshape(1, stat_count)], axis=1
    )
    merged = jnp.concatenate(
        [
            mixed_own.reshape(block_rows, head_dim).astype(jnp.bfloat16),
            fresh_columns,
            jnp.concatenate(
                [
                    split_three(own_stats),
                    jnp.zeros((1, stat_rows * head_dim - 6 * stat_count), jnp.bfloat16),
                ],
                axis=1,
            ).reshape(stat_rows, head_dim),
            jnp.zeros((spare_rows, head_dim), jnp.bfloat16),
        ],
        axis=0,
    )
    everything = lax.all_to_all(
        jnp.broadcast_to(merged[None], (groups,) + merged.shape), "grp", 0, 0, tiled=False
    )
    all_mixed = everything[:, :block_rows].astype(jnp.float32).reshape(
        heads, group_size, rows, head_dim
    )
    all_stats = join_three(
        everything[:, stat_at : stat_at + stat_rows].reshape(groups, -1)[:, : 6 * stat_count],
        2 * stat_count,
    )
    all_top = all_stats[:, :stat_count].reshape(heads, group_size, rows)
    all_total = all_stats[:, stat_count:].reshape(heads, group_size, rows)
    new_all = everything[:, block_rows:stat_at]
    new_keys = new_all[: groups // 2]
    new_values = new_all[groups // 2 :]
    attention_parts = (all_mixed, all_top, all_total, query, new_keys, new_values)

    targets = departing_target[:, 0]
    count_out = departing_slots.shape[0]
    order = jnp.arange(count_out, dtype=jnp.int32)
    earlier = (targets[:, None] == targets[None, :]) & (order[None, :] < order[:, None])
    place = jnp.sum(earlier.astype(jnp.int32), axis=1)
    live_slots = rows * pages
    capacity = (key_value_pages.shape[0] - live_slots) // homes
    lands = (targets[None, None, :] == jnp.arange(homes, dtype=jnp.int32)[:, None, None]) & (
        place[None, None, :] == jnp.arange(capacity, dtype=jnp.int32)[None, :, None]
    )
    filled = jnp.any(lands, axis=2)
    source_slot = jnp.sum(jnp.where(lands, departing_slots[None, None, :], 0), axis=2)

    page_slot = page_slot_table[request_index, lengths // page_size]
    offset = lengths % page_size
    mine = offset // slot_tokens == group_index
    token_local = offset % slot_tokens
    current = key_value_pages[page_slot, token_local]
    fresh = jnp.stack([new_keys, new_values], axis=0).transpose(2, 0, 1, 3)
    written = key_value_pages.at[page_slot, token_local].set(
        jnp.where(mine[:, None, None, None], fresh, current)
    )

    written = written.at[live_slots].set(jnp.zeros((), key_value_pages.dtype))
    outbound = written[jnp.where(filled, source_slot, live_slots)]
    outbound, attention_parts = lax.optimization_barrier((outbound, attention_parts))
    arrived = lax.all_to_all(outbound, "req", split_axis=0, concat_axis=0, tiled=True)
    attention = finish_attention(*attention_parts)
    migrated_pool = lax.dynamic_update_slice_in_dim(
        written,
        arrived.reshape((homes * capacity,) + key_value_pages.shape[1:]),
        live_slots,
        axis=0,
    )
    return (attention, migrated_pool)


def solution(mesh):
    in_specs = (
        P(None, "req"),
        P("req", "grp"),
        P("req", "grp", None),
        P(None, None, "grp"),
        P(),
        P("req", None),
        P("req", "grp", None, None, None),
        P("req"),
        P("req", None),
        P("req"),
        P("req", None),
    )
    out_specs = (P("req", None), P("req", "grp", None, None, None))
    return jax.shard_map(shards, mesh=mesh, in_specs=in_specs, out_specs=out_specs, check_vma=False)
```

```python
import math

import jax
import jax.numpy as jnp
from jax import lax
from jax.sharding import PartitionSpec as P

adapter_scale = 2.0
masked_score = -1e30


def split_three(value):
    first = lax.reduce_precision(value, exponent_bits=8, mantissa_bits=7)
    rest = value - first
    second = lax.reduce_precision(rest, exponent_bits=8, mantissa_bits=7)
    third = rest - second
    return jnp.concatenate([first, second, third], axis=-1).astype(jnp.bfloat16)


def join_three(parts, width):
    wide = parts.astype(jnp.float32)
    return wide[..., :width] + wide[..., width : 2 * width] + wide[..., 2 * width :]


def finish_attention(all_mixed, all_top, all_total, query, new_keys, new_values):
    rows, heads, group_size, head_dim = query.shape
    new_score = jnp.einsum(
        "ihgd,hid->hgi", query, new_keys, preferred_element_type=jnp.float32
    ) / math.sqrt(head_dim)
    top = jnp.maximum(all_top, new_score)
    old_scale = jnp.exp(all_top - top)
    new_weight = jnp.exp(new_score - top)
    total = all_total * old_scale + new_weight
    mixed = (
        all_mixed * old_scale[..., None]
        + new_weight[..., None] * new_values.astype(jnp.float32)[:, None, :, :]
    )
    attention = (mixed / total[..., None]).astype(jnp.bfloat16)
    return attention.transpose(2, 0, 1, 3).reshape(rows, -1)

def shards(
    normed_token_input,
    key_value_weight,
    adapter_down_weight,
    adapter_up_weight,
    adapter_index_rows,
    queries,
    key_value_pages,
    lengths,
    page_slot_table,
    departing_slots,
    departing_target,
):
    selected_adapter = adapter_index_rows[:, 0]
    request_index = jnp.arange(lengths.shape[0], dtype=jnp.int32)
    homes = lax.axis_size("req")
    groups = lax.axis_size("grp")
    home_index = lax.axis_index("req")
    group_index = lax.axis_index("grp")
    rows = lengths.shape[0]
    request_count = normed_token_input.shape[0]
    column_span = key_value_weight.shape[1]
    local_adapters = adapter_down_weight.shape[1]
    rank_width = adapter_down_weight.shape[2]
    rank_half = adapter_up_weight.shape[1]
    slot_tokens = key_value_pages.shape[1]
    heads = key_value_pages.shape[3]
    head_dim = key_value_pages.shape[4]
    key_width = heads * head_dim
    query_heads = queries.shape[1] // head_dim
    heads_per_target = query_heads // groups
    page_size = slot_tokens * groups
    pages = page_slot_table.shape[1]

    both = jnp.concatenate(
        [key_value_weight, adapter_down_weight.reshape(adapter_down_weight.shape[0], -1)], axis=1
    )
    by_home = normed_token_input.reshape(homes, rows, -1)
    products = jnp.einsum("hiw,wc->hic", by_home, both, preferred_element_type=jnp.float32)
    base_part = products[:, :, :column_span]
    down_all = products[:, :, column_span:].reshape(homes, rows, local_adapters, rank_width)
    local_choice = (selected_adapter - group_index * local_adapters).reshape(homes, rows)
    picker = local_choice[:, :, None] == jnp.arange(local_adapters, dtype=jnp.int32)[None, None, :]
    mid_part = jnp.sum(jnp.where(picker[..., None], down_all, 0.0), axis=2)
    partial = jnp.concatenate([base_part, mid_part], axis=2)
    resident_adapters = lax.dynamic_slice_in_dim(selected_adapter, home_index * rows, rows)
    up_weight_rows = adapter_up_weight[resident_adapters]
    summed = jnp.sum(lax.all_to_all(partial, "req", 0, 0, tiled=False), axis=0)
    base_resident = summed[:, :column_span]

    owner = resident_adapters // local_adapters
    is_value = group_index * column_span >= key_width

    live_slots = rows * pages
    live = key_value_pages[:live_slots, 0]
    keys = live[:, 0]
    values = live[:, 1]
    query = queries.reshape(rows, heads, -1, head_dim)
    group_size = query.shape[2]
    entry_of_slot = jnp.argmax(
        page_slot_table.reshape(1, -1) == jnp.arange(live_slots, dtype=jnp.int32)[:, None], axis=1
    )
    slot_request = entry_of_slot // pages
    slot_position = (entry_of_slot % pages) * page_size + group_index * slot_tokens
    valid = (slot_request[None, :] == request_index[:, None]) & (
        slot_position[None, :] < lengths[:, None]
    )
    valid = valid[None, None]
    scores = jnp.einsum(
        "ihgd,shd->hgis", query, keys, preferred_element_type=jnp.float32
    ) / math.sqrt(head_dim)
    scores = jnp.where(valid, scores, masked_score)
    local_top = jnp.max(scores, axis=3)
    weights = jnp.where(valid, jnp.exp(scores - local_top[..., None]), 0.0)
    local_total = jnp.sum(weights, axis=3)
    local_mixed = jnp.einsum(
        "hgis,shd->hgid", weights, values, preferred_element_type=jnp.float32
    )

    block_rows = heads_per_target * rows
    stat_count = heads_per_target * rows
    stat_rows = -(-6 * stat_count // head_dim)
    spare_rows = 8 - stat_rows
    stats = jnp.concatenate(
        [local_top.reshape(groups, stat_count), local_total.reshape(groups, stat_count)], axis=1
    )
    stat_pack = jnp.concatenate(
        [split_three(stats), jnp.zeros((groups, stat_rows * head_dim - 6 * stat_count), jnp.bfloat16)],
        axis=1,
    ).reshape(groups, stat_rows, head_dim)
    mid_rows = summed[:, column_span:].astype(jnp.bfloat16)
    parcel = jnp.concatenate(
        [
            local_mixed.reshape(groups, block_rows, head_dim).astype(jnp.bfloat16),
            jnp.broadcast_to(mid_rows[None], (groups,) + mid_rows.shape),
            stat_pack,
            jnp.zeros((groups, spare_rows, head_dim), jnp.bfloat16),
        ],
        axis=1,
    )
    received, up_weight_rows = lax.optimization_barrier(
        (lax.all_to_all(parcel, "grp", 0, 0, tiled=False), up_weight_rows)
    )
    stat_at = block_rows + rows
    shard_mixed = received[:, :block_rows].astype(jnp.float32).reshape(
        groups, heads_per_target, rows, head_dim
    )
    shard_stats = join_three(
        received[:, stat_at : stat_at + stat_rows].reshape(groups, -1)[:, : 6 * stat_count],
        2 * stat_count,
    )
    shard_top = shard_stats[:, :stat_count].reshape(groups, heads_per_target, rows)
    shard_total = shard_stats[:, stat_count:].reshape(groups, heads_per_target, rows)
    mid_spread = received[:, block_rows:stat_at]
    top_own = jnp.max(shard_top, axis=0)
    shard_scale = jnp.exp(shard_top - top_own[None])
    total_own = jnp.sum(shard_total * shard_scale, axis=0)
    mixed_own = jnp.sum(shard_mixed * shard_scale[..., None], axis=0)

    from_owner = owner[None, :, None] == jnp.arange(groups, dtype=jnp.int32)[:, None, None]
    mid_home = jnp.sum(
        jnp.where(from_owner, mid_spread.astype(jnp.float32), 0.0), axis=0
    ).astype(jnp.bfloat16)
    mid_used = jnp.where(is_value, mid_home[:, rank_half:], mid_home[:, :rank_half])
    adapter_update = jnp.einsum(
        "ir,irc->ic", mid_used, up_weight_rows, preferred_element_type=jnp.float32
    )
    fresh_columns = (base_resident + adapter_scale * adapter_update).astype(jnp.bfloat16)

    own_stats = jnp.concatenate(
        [top_own.reshape(1, stat_count), total_own.reshape(1, stat_count)], axis=1
    )
    merged = jnp.concatenate(
        [
            mixed_own.reshape(block_rows, head_dim).astype(jnp.bfloat16),
            fresh_columns,
            jnp.concatenate(
                [
                    split_three(own_stats),
                    jnp.zeros((1, stat_rows * head_dim - 6 * stat_count), jnp.bfloat16),
                ],
                axis=1,
            ).reshape(stat_rows, head_dim),
            jnp.zeros((spare_rows, head_dim), jnp.bfloat16),
        ],
        axis=0,
    )
    everything = lax.all_to_all(
        jnp.broadcast_to(merged[None], (groups,) + merged.shape), "grp", 0, 0, tiled=False
    )
    all_mixed = everything[:, :block_rows].astype(jnp.float32).reshape(
        heads, group_size, rows, head_dim
    )
    all_stats = join_three(
        everything[:, stat_at : stat_at + stat_rows].reshape(groups, -1)[:, : 6 * stat_count],
        2 * stat_count,
    )
    all_top = all_stats[:, :stat_count].reshape(heads, group_size, rows)
    all_total = all_stats[:, stat_count:].reshape(heads, group_size, rows)
    new_all = everything[:, block_rows:stat_at]
    new_keys = new_all[: groups // 2]
    new_values = new_all[groups // 2 :]
    attention_parts = (all_mixed, all_top, all_total, query, new_keys, new_values)

    targets = departing_target[:, 0]
    count_out = departing_slots.shape[0]
    order = jnp.arange(count_out, dtype=jnp.int32)
    earlier = (targets[:, None] == targets[None, :]) & (order[None, :] < order[:, None])
    place = jnp.sum(earlier.astype(jnp.int32), axis=1)
    live_slots = rows * pages
    capacity = (key_value_pages.shape[0] - live_slots) // homes
    lands = (targets[None, None, :] == jnp.arange(homes, dtype=jnp.int32)[:, None, None]) & (
        place[None, None, :] == jnp.arange(capacity, dtype=jnp.int32)[None, :, None]
    )
    filled = jnp.any(lands, axis=2)
    source_slot = jnp.sum(jnp.where(lands, departing_slots[None, None, :], 0), axis=2)

    page_slot = page_slot_table[request_index, lengths // page_size]
    offset = lengths % page_size
    mine = offset // slot_tokens == group_index
    token_local = offset % slot_tokens
    current = key_value_pages[page_slot, token_local]
    fresh = jnp.stack([new_keys, new_values], axis=0).transpose(2, 0, 1, 3)
    written = key_value_pages.at[page_slot, token_local].set(
        jnp.where(mine[:, None, None, None], fresh, current)
    )

    written = written.at[live_slots].set(jnp.zeros((), key_value_pages.dtype))
    outbound = written[jnp.where(filled, source_slot, live_slots)]
    outbound, attention_parts = lax.optimization_barrier((outbound, attention_parts))
    arrived = lax.all_to_all(outbound, "req", split_axis=0, concat_axis=0, tiled=True)
    attention = finish_attention(*attention_parts)
    migrated_pool = lax.dynamic_update_slice_in_dim(
        written,
        arrived.reshape((homes * capacity,) + key_value_pages.shape[1:]),
        live_slots,
        axis=0,
    )
    return (attention, migrated_pool)


def solution(mesh):
    in_specs = (
        P(None, "req"),
        P("req", "grp"),
        P("req", "grp", None),
        P(None, None, "grp"),
        P(),
        P("req", None),
        P("req", "grp", None, None, None),
        P("req"),
        P("req", None),
        P("req"),
        P("req", None),
    )
    out_specs = (P("req", None), P("req", "grp", None, None, None))
    return jax.shard_map(shards, mesh=mesh, in_specs=in_specs, out_specs=out_specs, check_vma=False)
```

```python
import math

import jax
import jax.numpy as jnp
from jax import lax
from jax.sharding import PartitionSpec as P

adapter_scale = 2.0
masked_score = -1e30


def split_three(value):
    first = lax.reduce_precision(value, exponent_bits=8, mantissa_bits=7)
    rest = value - first
    second = lax.reduce_precision(rest, exponent_bits=8, mantissa_bits=7)
    third = rest - second
    return jnp.concatenate([first, second, third], axis=-1).astype(jnp.bfloat16)


def join_three(parts, width):
    wide = parts.astype(jnp.float32)
    return wide[..., :width] + wide[..., width : 2 * width] + wide[..., 2 * width :]


def finish_attention(all_mixed, all_top, all_total, query, new_keys, new_values):
    rows, heads, group_size, head_dim = query.shape
    new_score = jnp.einsum(
        "ihgd,hid->hgi", query, new_keys, preferred_element_type=jnp.float32
    ) / math.sqrt(head_dim)
    top = jnp.maximum(all_top, new_score)
    old_scale = jnp.exp(all_top - top)
    new_weight = jnp.exp(new_score - top)
    total = all_total * old_scale + new_weight
    mixed = (
        all_mixed * old_scale[..., None]
        + new_weight[..., None] * new_values.astype(jnp.float32)[:, None, :, :]
    )
    attention = (mixed / total[..., None]).astype(jnp.bfloat16)
    return attention.transpose(2, 0, 1, 3).reshape(rows, -1)

def shards(
    normed_token_input,
    key_value_weight,
    adapter_down_weight,
    adapter_up_weight,
    adapter_index_rows,
    queries,
    key_value_pages,
    lengths,
    page_slot_table,
    departing_slots,
    departing_target,
):
    selected_adapter = adapter_index_rows[:, 0]
    request_index = jnp.arange(lengths.shape[0], dtype=jnp.int32)
    homes = lax.axis_size("req")
    groups = lax.axis_size("grp")
    home_index = lax.axis_index("req")
    group_index = lax.axis_index("grp")
    rows = lengths.shape[0]
    request_count = normed_token_input.shape[0]
    column_span = key_value_weight.shape[1]
    local_adapters = adapter_down_weight.shape[1]
    rank_width = adapter_down_weight.shape[2]
    rank_half = adapter_up_weight.shape[1]
    slot_tokens = key_value_pages.shape[1]
    heads = key_value_pages.shape[3]
    head_dim = key_value_pages.shape[4]
    key_width = heads * head_dim
    query_heads = queries.shape[1] // head_dim
    heads_per_target = query_heads // groups
    page_size = slot_tokens * groups
    pages = page_slot_table.shape[1]

    both = jnp.concatenate(
        [key_value_weight, adapter_down_weight.reshape(adapter_down_weight.shape[0], -1)], axis=1
    )
    products = jnp.dot(normed_token_input, both, preferred_element_type=jnp.float32).reshape(
        homes, rows, -1
    )
    base_part = products[:, :, :column_span]
    down_all = products[:, :, column_span:].reshape(homes, rows, local_adapters, rank_width)
    local_choice = (selected_adapter - group_index * local_adapters).reshape(homes, rows)
    picker = local_choice[:, :, None] == jnp.arange(local_adapters, dtype=jnp.int32)[None, None, :]
    mid_part = jnp.sum(jnp.where(picker[..., None], down_all, 0.0), axis=2)
    partial = jnp.concatenate([base_part, mid_part], axis=2)
    resident_adapters = lax.dynamic_slice_in_dim(selected_adapter, home_index * rows, rows)
    up_weight_rows = adapter_up_weight[resident_adapters]
    summed = jnp.sum(lax.all_to_all(partial, "req", 0, 0, tiled=False), axis=0)
    base_resident = summed[:, :column_span]

    owner = resident_adapters // local_adapters
    is_value = group_index * column_span >= key_width

    live_slots = rows * pages
    live = key_value_pages[:live_slots, 0]
    keys = live[:, 0]
    values = live[:, 1]
    query = queries.reshape(rows, heads, -1, head_dim)
    group_size = query.shape[2]
    entry_of_slot = jnp.argmax(
        page_slot_table.reshape(1, -1) == jnp.arange(live_slots, dtype=jnp.int32)[:, None], axis=1
    )
    slot_request = entry_of_slot // pages
    slot_position = (entry_of_slot % pages) * page_size + group_index * slot_tokens
    valid = (slot_request[None, :] == request_index[:, None]) & (
        slot_position[None, :] < lengths[:, None]
    )
    valid = valid[None, None]
    scores = jnp.einsum(
        "ihgd,shd->hgis", query, keys, preferred_element_type=jnp.float32
    ) / math.sqrt(head_dim)
    scores = jnp.where(valid, scores, masked_score)
    local_top = jnp.max(scores, axis=3)
    weights = jnp.where(valid, jnp.exp(scores - local_top[..., None]), 0.0)
    local_total = jnp.sum(weights, axis=3)
    local_mixed = jnp.einsum(
        "hgis,shd->hgid", weights, values, preferred_element_type=jnp.float32
    )

    block_rows = heads_per_target * rows
    stat_count = heads_per_target * rows
    stat_rows = -(-6 * stat_count // head_dim)
    spare_rows = 8 - stat_rows
    stats = jnp.concatenate(
        [local_top.reshape(groups, stat_count), local_total.reshape(groups, stat_count)], axis=1
    )
    stat_pack = jnp.concatenate(
        [split_three(stats), jnp.zeros((groups, stat_rows * head_dim - 6 * stat_count), jnp.bfloat16)],
        axis=1,
    ).reshape(groups, stat_rows, head_dim)
    mid_rows = summed[:, column_span:].astype(jnp.bfloat16)
    parcel = jnp.concatenate(
        [
            local_mixed.reshape(groups, block_rows, head_dim).astype(jnp.bfloat16),
            jnp.broadcast_to(mid_rows[None], (groups,) + mid_rows.shape),
            stat_pack,
            jnp.zeros((groups, spare_rows, head_dim), jnp.bfloat16),
        ],
        axis=1,
    )
    received, up_weight_rows = lax.optimization_barrier(
        (lax.all_to_all(parcel, "grp", 0, 0, tiled=False), up_weight_rows)
    )
    stat_at = block_rows + rows
    shard_mixed = received[:, :block_rows].astype(jnp.float32).reshape(
        groups, heads_per_target, rows, head_dim
    )
    shard_stats = join_three(
        received[:, stat_at : stat_at + stat_rows].reshape(groups, -1)[:, : 6 * stat_count],
        2 * stat_count,
    )
    shard_top = shard_stats[:, :stat_count].reshape(groups, heads_per_target, rows)
    shard_total = shard_stats[:, stat_count:].reshape(groups, heads_per_target, rows)
    mid_spread = received[:, block_rows:stat_at]
    top_own = jnp.max(shard_top, axis=0)
    shard_scale = jnp.exp(shard_top - top_own[None])
    total_own = jnp.sum(shard_total * shard_scale, axis=0)
    mixed_own = jnp.sum(shard_mixed * shard_scale[..., None], axis=0)

    from_owner = owner[None, :, None] == jnp.arange(groups, dtype=jnp.int32)[:, None, None]
    mid_home = jnp.sum(
        jnp.where(from_owner, mid_spread.astype(jnp.float32), 0.0), axis=0
    ).astype(jnp.bfloat16)
    mid_used = jnp.where(is_value, mid_home[:, rank_half:], mid_home[:, :rank_half])
    adapter_update = jnp.einsum(
        "ir,irc->ic", mid_used, up_weight_rows, preferred_element_type=jnp.float32
    )
    fresh_columns = (base_resident + adapter_scale * adapter_update).astype(jnp.bfloat16)

    own_stats = jnp.concatenate(
        [top_own.reshape(1, stat_count), total_own.reshape(1, stat_count)], axis=1
    )
    merged = jnp.concatenate(
        [
            mixed_own.reshape(block_rows, head_dim).astype(jnp.bfloat16),
            fresh_columns,
            jnp.concatenate(
                [
                    split_three(own_stats),
                    jnp.zeros((1, stat_rows * head_dim - 6 * stat_count), jnp.bfloat16),
                ],
                axis=1,
            ).reshape(stat_rows, head_dim),
            jnp.zeros((spare_rows, head_dim), jnp.bfloat16),
        ],
        axis=0,
    )
    everything = lax.all_to_all(
        jnp.broadcast_to(merged[None], (groups,) + merged.shape), "grp", 0, 0, tiled=False
    )
    all_mixed = everything[:, :block_rows].astype(jnp.float32).reshape(
        heads, group_size, rows, head_dim
    )
    all_stats = join_three(
        everything[:, stat_at : stat_at + stat_rows].reshape(groups, -1)[:, : 6 * stat_count],
        2 * stat_count,
    )
    all_top = all_stats[:, :stat_count].reshape(heads, group_size, rows)
    all_total = all_stats[:, stat_count:].reshape(heads, group_size, rows)
    new_all = everything[:, block_rows:stat_at]
    new_keys = new_all[: groups // 2]
    new_values = new_all[groups // 2 :]
    attention_parts = (all_mixed, all_top, all_total, query, new_keys, new_values)

    targets = departing_target[:, 0]
    count_out = departing_slots.shape[0]
    order = jnp.arange(count_out, dtype=jnp.int32)
    earlier = (targets[:, None] == targets[None, :]) & (order[None, :] < order[:, None])
    place = jnp.sum(earlier.astype(jnp.int32), axis=1)
    live_slots = rows * pages
    capacity = (key_value_pages.shape[0] - live_slots) // homes
    lands = (targets[None, None, :] == jnp.arange(homes, dtype=jnp.int32)[:, None, None]) & (
        place[None, None, :] == jnp.arange(capacity, dtype=jnp.int32)[None, :, None]
    )
    filled = jnp.any(lands, axis=2)
    source_slot = jnp.sum(jnp.where(lands, departing_slots[None, None, :], 0), axis=2)

    page_slot = page_slot_table[request_index, lengths // page_size]
    offset = lengths % page_size
    mine = offset // slot_tokens == group_index
    token_local = offset % slot_tokens
    current = key_value_pages[page_slot, token_local]
    fresh = jnp.stack([new_keys, new_values], axis=0).transpose(2, 0, 1, 3)
    written = key_value_pages.at[page_slot, token_local].set(
        jnp.where(mine[:, None, None, None], fresh, current)
    )

    written = written.at[live_slots].set(jnp.zeros((), key_value_pages.dtype))
    outbound = written[jnp.where(filled, source_slot, live_slots)]
    outbound, attention_parts = lax.optimization_barrier((outbound, attention_parts))
    arrived = lax.all_to_all(outbound, "req", split_axis=0, concat_axis=0, tiled=True)
    attention = finish_attention(*attention_parts)
    migrated_pool = lax.dynamic_update_slice_in_dim(
        written,
        arrived.reshape((homes * capacity,) + key_value_pages.shape[1:]),
        live_slots,
        axis=0,
    )
    return (attention, migrated_pool)


def solution(mesh):
    in_specs = (
        P(None, "req"),
        P("req", "grp"),
        P("req", "grp", None),
        P(None, None, "grp"),
        P(),
        P("req", None),
        P("req", "grp", None, None, None),
        P("req"),
        P("req", None),
        P("req"),
        P("req", None),
    )
    out_specs = (P("req", None), P("req", "grp", None, None, None))
    return jax.shard_map(shards, mesh=mesh, in_specs=in_specs, out_specs=out_specs, check_vma=False)
```

```python
import math

import jax
import jax.numpy as jnp
from jax import lax
from jax.sharding import PartitionSpec as P

adapter_scale = 2.0
masked_score = -1e30


def split_three(value):
    first = lax.reduce_precision(value, exponent_bits=8, mantissa_bits=7)
    rest = value - first
    second = lax.reduce_precision(rest, exponent_bits=8, mantissa_bits=7)
    third = rest - second
    return jnp.concatenate([first, second, third], axis=-1).astype(jnp.bfloat16)


def join_three(parts, width):
    wide = parts.astype(jnp.float32)
    return wide[..., :width] + wide[..., width : 2 * width] + wide[..., 2 * width :]


def finish_attention(all_mixed, all_top, all_total, query, new_keys, new_values):
    rows, heads, group_size, head_dim = query.shape
    new_score = jnp.einsum(
        "ihgd,hid->hgi", query, new_keys, preferred_element_type=jnp.float32
    ) / math.sqrt(head_dim)
    top = jnp.maximum(all_top, new_score)
    old_scale = jnp.exp(all_top - top)
    new_weight = jnp.exp(new_score - top)
    total = all_total * old_scale + new_weight
    mixed = (
        all_mixed * old_scale[..., None]
        + new_weight[..., None] * new_values.astype(jnp.float32)[:, None, :, :]
    )
    attention = (mixed / total[..., None]).astype(jnp.bfloat16)
    return attention.transpose(2, 0, 1, 3).reshape(rows, -1)

def shards(
    normed_token_input,
    key_value_weight,
    adapter_down_weight,
    adapter_up_weight,
    adapter_index_rows,
    queries,
    key_value_pages,
    lengths,
    page_slot_table,
    departing_slots,
    departing_target,
):
    selected_adapter = adapter_index_rows[:, 0]
    request_index = jnp.arange(lengths.shape[0], dtype=jnp.int32)
    homes = lax.axis_size("req")
    groups = lax.axis_size("grp")
    home_index = lax.axis_index("req")
    group_index = lax.axis_index("grp")
    rows = lengths.shape[0]
    request_count = normed_token_input.shape[0]
    column_span = key_value_weight.shape[1]
    local_adapters = adapter_down_weight.shape[1]
    rank_width = adapter_down_weight.shape[2]
    rank_half = adapter_up_weight.shape[1]
    slot_tokens = key_value_pages.shape[1]
    heads = key_value_pages.shape[3]
    head_dim = key_value_pages.shape[4]
    key_width = heads * head_dim
    query_heads = queries.shape[1] // head_dim
    heads_per_target = query_heads // groups
    page_size = slot_tokens * groups
    pages = page_slot_table.shape[1]

    both = jnp.concatenate(
        [key_value_weight, adapter_down_weight.reshape(adapter_down_weight.shape[0], -1)], axis=1
    )
    products = jnp.dot(normed_token_input, both, preferred_element_type=jnp.float32).reshape(
        homes, rows, -1
    )
    base_part = products[:, :, :column_span]
    down_all = products[:, :, column_span:].reshape(homes, rows, local_adapters, rank_width)
    local_choice = (selected_adapter - group_index * local_adapters).reshape(homes, rows)
    picker = local_choice[:, :, None] == jnp.arange(local_adapters, dtype=jnp.int32)[None, None, :]
    mid_part = jnp.sum(jnp.where(picker[..., None], down_all, 0.0), axis=2)
    partial = jnp.concatenate([base_part, mid_part], axis=2)
    resident_adapters = lax.dynamic_slice_in_dim(selected_adapter, home_index * rows, rows)
    up_weight_rows = adapter_up_weight[resident_adapters]
    summed = jnp.sum(lax.all_to_all(partial, "req", 0, 0, tiled=False), axis=0)
    base_resident = summed[:, :column_span]

    owner = resident_adapters // local_adapters
    is_value = group_index * column_span >= key_width

    live_slots = rows * pages
    live = key_value_pages[:live_slots, 0]
    keys = live[:, 0]
    values = live[:, 1]
    query = queries.reshape(rows, heads, -1, head_dim)
    group_size = query.shape[2]
    entry_of_slot = jnp.argmax(
        page_slot_table.reshape(1, -1) == jnp.arange(live_slots, dtype=jnp.int32)[:, None], axis=1
    )
    slot_request = entry_of_slot // pages
    slot_position = (entry_of_slot % pages) * page_size + group_index * slot_tokens
    valid = (slot_request[None, :] == request_index[:, None]) & (
        slot_position[None, :] < lengths[:, None]
    )
    valid = valid[None, None]
    scores = jnp.einsum(
        "ihgd,shd->hgis", query, keys, preferred_element_type=jnp.float32
    ) / math.sqrt(head_dim)
    scores = jnp.where(valid, scores, masked_score)
    local_top = jnp.max(scores, axis=3)
    weights = jnp.where(valid, jnp.exp(scores - local_top[..., None]), 0.0)
    local_total = jnp.sum(weights, axis=3)
    local_mixed = jnp.einsum(
        "hgis,shd->hgid", weights, values, preferred_element_type=jnp.float32
    )

    block_rows = heads_per_target * rows
    stat_count = heads_per_target * rows
    stat_rows = -(-6 * stat_count // head_dim)
    spare_rows = 8 - stat_rows
    stats = jnp.concatenate(
        [local_top.reshape(groups, stat_count), local_total.reshape(groups, stat_count)], axis=1
    )
    stat_pack = jnp.concatenate(
        [split_three(stats), jnp.zeros((groups, stat_rows * head_dim - 6 * stat_count), jnp.bfloat16)],
        axis=1,
    ).reshape(groups, stat_rows, head_dim)
    mid_rows = summed[:, column_span:].astype(jnp.bfloat16)
    parcel = jnp.concatenate(
        [
            local_mixed.reshape(groups, block_rows, head_dim).astype(jnp.bfloat16),
            jnp.zeros((groups,) + mid_rows.shape, jnp.bfloat16),
            stat_pack,
            jnp.zeros((groups, spare_rows, head_dim), jnp.bfloat16),
        ],
        axis=1,
    )
    parcel = lax.dynamic_update_slice_in_dim(
        parcel, jnp.broadcast_to(mid_rows[None], (groups,) + mid_rows.shape), block_rows, axis=1
    )
    received, up_weight_rows = lax.optimization_barrier(
        (lax.all_to_all(parcel, "grp", 0, 0, tiled=False), up_weight_rows)
    )
    stat_at = block_rows + rows
    shard_mixed = received[:, :block_rows].astype(jnp.float32).reshape(
        groups, heads_per_target, rows, head_dim
    )
    shard_stats = join_three(
        received[:, stat_at : stat_at + stat_rows].reshape(groups, -1)[:, : 6 * stat_count],
        2 * stat_count,
    )
    shard_top = shard_stats[:, :stat_count].reshape(groups, heads_per_target, rows)
    shard_total = shard_stats[:, stat_count:].reshape(groups, heads_per_target, rows)
    mid_spread = received[:, block_rows:stat_at]
    top_own = jnp.max(shard_top, axis=0)
    shard_scale = jnp.exp(shard_top - top_own[None])
    total_own = jnp.sum(shard_total * shard_scale, axis=0)
    mixed_own = jnp.sum(shard_mixed * shard_scale[..., None], axis=0)

    from_owner = owner[None, :, None] == jnp.arange(groups, dtype=jnp.int32)[:, None, None]
    mid_home = jnp.sum(
        jnp.where(from_owner, mid_spread.astype(jnp.float32), 0.0), axis=0
    ).astype(jnp.bfloat16)
    mid_used = jnp.where(is_value, mid_home[:, rank_half:], mid_home[:, :rank_half])
    adapter_update = jnp.einsum(
        "ir,irc->ic", mid_used, up_weight_rows, preferred_element_type=jnp.float32
    )
    fresh_columns = (base_resident + adapter_scale * adapter_update).astype(jnp.bfloat16)

    own_stats = jnp.concatenate(
        [top_own.reshape(1, stat_count), total_own.reshape(1, stat_count)], axis=1
    )
    merged = jnp.concatenate(
        [
            mixed_own.reshape(block_rows, head_dim).astype(jnp.bfloat16),
            fresh_columns,
            jnp.concatenate(
                [
                    split_three(own_stats),
                    jnp.zeros((1, stat_rows * head_dim - 6 * stat_count), jnp.bfloat16),
                ],
                axis=1,
            ).reshape(stat_rows, head_dim),
            jnp.zeros((spare_rows, head_dim), jnp.bfloat16),
        ],
        axis=0,
    )
    everything = lax.all_to_all(
        jnp.broadcast_to(merged[None], (groups,) + merged.shape), "grp", 0, 0, tiled=False
    )
    all_mixed = everything[:, :block_rows].astype(jnp.float32).reshape(
        heads, group_size, rows, head_dim
    )
    all_stats = join_three(
        everything[:, stat_at : stat_at + stat_rows].reshape(groups, -1)[:, : 6 * stat_count],
        2 * stat_count,
    )
    all_top = all_stats[:, :stat_count].reshape(heads, group_size, rows)
    all_total = all_stats[:, stat_count:].reshape(heads, group_size, rows)
    new_all = everything[:, block_rows:stat_at]
    new_keys = new_all[: groups // 2]
    new_values = new_all[groups // 2 :]
    attention_parts = (all_mixed, all_top, all_total, query, new_keys, new_values)

    targets = departing_target[:, 0]
    count_out = departing_slots.shape[0]
    order = jnp.arange(count_out, dtype=jnp.int32)
    earlier = (targets[:, None] == targets[None, :]) & (order[None, :] < order[:, None])
    place = jnp.sum(earlier.astype(jnp.int32), axis=1)
    live_slots = rows * pages
    capacity = (key_value_pages.shape[0] - live_slots) // homes
    lands = (targets[None, None, :] == jnp.arange(homes, dtype=jnp.int32)[:, None, None]) & (
        place[None, None, :] == jnp.arange(capacity, dtype=jnp.int32)[None, :, None]
    )
    filled = jnp.any(lands, axis=2)
    source_slot = jnp.sum(jnp.where(lands, departing_slots[None, None, :], 0), axis=2)

    page_slot = page_slot_table[request_index, lengths // page_size]
    offset = lengths % page_size
    mine = offset // slot_tokens == group_index
    token_local = offset % slot_tokens
    fresh = jnp.stack([new_keys, new_values], axis=0).transpose(2, 0, 1, 3)
    written = key_value_pages.at[
        jnp.where(mine, page_slot, key_value_pages.shape[0]), token_local
    ].set(fresh, mode="drop")

    written = written.at[live_slots].set(jnp.zeros((), key_value_pages.dtype))
    outbound = written[jnp.where(filled, source_slot, live_slots)]
    outbound, attention_parts = lax.optimization_barrier((outbound, attention_parts))
    arrived = lax.all_to_all(outbound, "req", split_axis=0, concat_axis=0, tiled=True)
    attention = finish_attention(*attention_parts)
    migrated_pool = lax.dynamic_update_slice_in_dim(
        written,
        arrived.reshape((homes * capacity,) + key_value_pages.shape[1:]),
        live_slots,
        axis=0,
    )
    return (attention, migrated_pool)


def solution(mesh):
    in_specs = (
        P(None, "req"),
        P("req", "grp"),
        P("req", "grp", None),
        P(None, None, "grp"),
        P(),
        P("req", None),
        P("req", "grp", None, None, None),
        P("req"),
        P("req", None),
        P("req"),
        P("req", None),
    )
    out_specs = (P("req", None), P("req", "grp", None, None, None))
    return jax.shard_map(shards, mesh=mesh, in_specs=in_specs, out_specs=out_specs, check_vma=False)
```

```python
import math

import jax
import jax.numpy as jnp
from jax import lax
from jax.sharding import PartitionSpec as P

adapter_scale = 2.0
masked_score = -1e30


def split_three(value):
    first = lax.reduce_precision(value, exponent_bits=8, mantissa_bits=7)
    rest = value - first
    second = lax.reduce_precision(rest, exponent_bits=8, mantissa_bits=7)
    third = rest - second
    return jnp.concatenate([first, second, third], axis=-1).astype(jnp.bfloat16)


def join_three(parts, width):
    wide = parts.astype(jnp.float32)
    return wide[..., :width] + wide[..., width : 2 * width] + wide[..., 2 * width :]


def finish_attention(all_mixed, all_top, all_total, query, new_keys, new_values):
    rows, heads, group_size, head_dim = query.shape
    new_score = jnp.einsum(
        "ihgd,hid->hgi", query, new_keys, preferred_element_type=jnp.float32
    ) / math.sqrt(head_dim)
    top = jnp.maximum(all_top, new_score)
    old_scale = jnp.exp(all_top - top)
    new_weight = jnp.exp(new_score - top)
    total = all_total * old_scale + new_weight
    mixed = (
        all_mixed * old_scale[..., None]
        + new_weight[..., None] * new_values.astype(jnp.float32)[:, None, :, :]
    )
    attention = (mixed / total[..., None]).astype(jnp.bfloat16)
    return attention.transpose(2, 0, 1, 3).reshape(rows, -1)

def shards(
    normed_token_input,
    key_value_weight,
    adapter_down_weight,
    adapter_up_weight,
    adapter_index_rows,
    queries,
    key_value_pages,
    lengths,
    page_slot_table,
    departing_slots,
    departing_target,
):
    selected_adapter = adapter_index_rows[:, 0]
    request_index = jnp.arange(lengths.shape[0], dtype=jnp.int32)
    homes = lax.axis_size("req")
    groups = lax.axis_size("grp")
    home_index = lax.axis_index("req")
    group_index = lax.axis_index("grp")
    rows = lengths.shape[0]
    request_count = normed_token_input.shape[0]
    column_span = key_value_weight.shape[1]
    local_adapters = adapter_down_weight.shape[1]
    rank_width = adapter_down_weight.shape[2]
    rank_half = adapter_up_weight.shape[1]
    slot_tokens = key_value_pages.shape[1]
    heads = key_value_pages.shape[3]
    head_dim = key_value_pages.shape[4]
    key_width = heads * head_dim
    query_heads = queries.shape[1] // head_dim
    heads_per_target = query_heads // groups
    page_size = slot_tokens * groups
    pages = page_slot_table.shape[1]

    both = jnp.concatenate(
        [key_value_weight, adapter_down_weight.reshape(adapter_down_weight.shape[0], -1)], axis=1
    )
    products = jnp.dot(normed_token_input, both, preferred_element_type=jnp.float32).reshape(
        homes, rows, -1
    )
    base_part = products[:, :, :column_span]
    down_all = products[:, :, column_span:].reshape(homes, rows, local_adapters, rank_width)
    local_choice = (selected_adapter - group_index * local_adapters).reshape(homes, rows)
    picker = local_choice[:, :, None] == jnp.arange(local_adapters, dtype=jnp.int32)[None, None, :]
    mid_part = jnp.sum(jnp.where(picker[..., None], down_all, 0.0), axis=2)
    partial = jnp.concatenate([base_part, mid_part], axis=2)
    resident_adapters = lax.dynamic_slice_in_dim(selected_adapter, home_index * rows, rows)
    up_weight_rows = adapter_up_weight[resident_adapters]
    summed = jnp.sum(lax.all_to_all(partial, "req", 0, 0, tiled=False), axis=0)
    base_resident = summed[:, :column_span]

    owner = resident_adapters // local_adapters
    is_value = group_index * column_span >= key_width

    live_slots = rows * pages
    live = key_value_pages[:live_slots, 0]
    keys = live[:, 0]
    values = live[:, 1]
    query = queries.reshape(rows, heads, -1, head_dim)
    group_size = query.shape[2]
    entry_of_slot = jnp.argmax(
        page_slot_table.reshape(1, -1) == jnp.arange(live_slots, dtype=jnp.int32)[:, None], axis=1
    )
    slot_request = entry_of_slot // pages
    slot_position = (entry_of_slot % pages) * page_size + group_index * slot_tokens
    valid = (slot_request[None, :] == request_index[:, None]) & (
        slot_position[None, :] < lengths[:, None]
    )
    valid = valid[None, None]
    scores = jnp.einsum(
        "ihgd,shd->hgis", query, keys, preferred_element_type=jnp.float32
    ) / math.sqrt(head_dim)
    scores = jnp.where(valid, scores, masked_score)
    local_top = jnp.max(scores, axis=3)
    weights = jnp.where(valid, jnp.exp(scores - local_top[..., None]), 0.0)
    local_total = jnp.sum(weights, axis=3)
    local_mixed = jnp.einsum(
        "hgis,shd->hgid", weights, values, preferred_element_type=jnp.float32
    )

    block_rows = heads_per_target * rows
    stat_count = heads_per_target * rows
    stat_rows = -(-6 * stat_count // head_dim)
    spare_rows = 8 - stat_rows
    stats = jnp.concatenate(
        [local_top.reshape(groups, stat_count), local_total.reshape(groups, stat_count)], axis=1
    )
    stat_pack = jnp.concatenate(
        [split_three(stats), jnp.zeros((groups, stat_rows * head_dim - 6 * stat_count), jnp.bfloat16)],
        axis=1,
    ).reshape(groups, stat_rows, head_dim)
    mid_rows = summed[:, column_span:].astype(jnp.bfloat16)
    parcel = jnp.concatenate(
        [
            local_mixed.reshape(groups, block_rows, head_dim).astype(jnp.bfloat16),
            jnp.broadcast_to(mid_rows[None], (groups,) + mid_rows.shape),
            stat_pack,
            jnp.zeros((groups, spare_rows, head_dim), jnp.bfloat16),
        ],
        axis=1,
    )
    received, up_weight_rows = lax.optimization_barrier(
        (lax.all_to_all(parcel, "grp", 0, 0, tiled=False), up_weight_rows)
    )
    stat_at = block_rows + rows
    shard_mixed = received[:, :block_rows].astype(jnp.float32).reshape(
        groups, heads_per_target, rows, head_dim
    )
    shard_stats = join_three(
        received[:, stat_at : stat_at + stat_rows].reshape(groups, -1)[:, : 6 * stat_count],
        2 * stat_count,
    )
    shard_top = shard_stats[:, :stat_count].reshape(groups, heads_per_target, rows)
    shard_total = shard_stats[:, stat_count:].reshape(groups, heads_per_target, rows)
    mid_spread = received[:, block_rows:stat_at]
    top_own = jnp.max(shard_top, axis=0)
    shard_scale = jnp.exp(shard_top - top_own[None])
    total_own = jnp.sum(shard_total * shard_scale, axis=0)
    mixed_own = jnp.sum(shard_mixed * shard_scale[..., None], axis=0)

    from_owner = owner[None, :, None] == jnp.arange(groups, dtype=jnp.int32)[:, None, None]
    mid_home = jnp.sum(
        jnp.where(from_owner, mid_spread.astype(jnp.float32), 0.0), axis=0
    ).astype(jnp.bfloat16)
    mid_used = jnp.where(is_value, mid_home[:, rank_half:], mid_home[:, :rank_half])
    adapter_update = jnp.einsum(
        "ir,irc->ic", mid_used, up_weight_rows, preferred_element_type=jnp.float32
    )
    fresh_columns = (base_resident + adapter_scale * adapter_update).astype(jnp.bfloat16)

    own_stats = jnp.concatenate(
        [top_own.reshape(1, stat_count), total_own.reshape(1, stat_count)], axis=1
    )
    merged = jnp.concatenate(
        [
            mixed_own.reshape(block_rows, head_dim).astype(jnp.bfloat16),
            fresh_columns,
            jnp.concatenate(
                [
                    split_three(own_stats),
                    jnp.zeros((1, stat_rows * head_dim - 6 * stat_count), jnp.bfloat16),
                ],
                axis=1,
            ).reshape(stat_rows, head_dim),
            jnp.zeros((spare_rows, head_dim), jnp.bfloat16),
        ],
        axis=0,
    )
    everything = lax.all_to_all(
        jnp.broadcast_to(merged[None], (groups,) + merged.shape), "grp", 0, 0, tiled=False
    )
    all_mixed = everything[:, :block_rows].astype(jnp.float32).reshape(
        heads, group_size, rows, head_dim
    )
    all_stats = join_three(
        everything[:, stat_at : stat_at + stat_rows].reshape(groups, -1)[:, : 6 * stat_count],
        2 * stat_count,
    )
    all_top = all_stats[:, :stat_count].reshape(heads, group_size, rows)
    all_total = all_stats[:, stat_count:].reshape(heads, group_size, rows)
    new_all = everything[:, block_rows:stat_at]
    new_keys = new_all[: groups // 2]
    new_values = new_all[groups // 2 :]
    attention_parts = (all_mixed, all_top, all_total, query, new_keys, new_values)

    targets = departing_target[:, 0]
    count_out = departing_slots.shape[0]
    order = jnp.arange(count_out, dtype=jnp.int32)
    earlier = (targets[:, None] == targets[None, :]) & (order[None, :] < order[:, None])
    place = jnp.sum(earlier.astype(jnp.int32), axis=1)
    live_slots = rows * pages
    capacity = (key_value_pages.shape[0] - live_slots) // homes
    lands = (targets[None, None, :] == jnp.arange(homes, dtype=jnp.int32)[:, None, None]) & (
        place[None, None, :] == jnp.arange(capacity, dtype=jnp.int32)[None, :, None]
    )
    filled = jnp.any(lands, axis=2)
    source_slot = jnp.sum(jnp.where(lands, departing_slots[None, None, :], 0), axis=2)

    page_slot = page_slot_table[request_index, lengths // page_size]
    offset = lengths % page_size
    mine = offset // slot_tokens == group_index
    token_local = offset % slot_tokens
    fresh = jnp.stack([new_keys, new_values], axis=0).transpose(2, 0, 1, 3)
    written = key_value_pages.at[
        jnp.where(mine, page_slot, key_value_pages.shape[0]), token_local
    ].set(fresh, mode="drop")

    written = written.at[live_slots].set(jnp.zeros((), key_value_pages.dtype))
    outbound = written[jnp.where(filled, source_slot, live_slots)]
    outbound, attention_parts = lax.optimization_barrier((outbound, attention_parts))
    arrived = lax.all_to_all(outbound, "req", split_axis=0, concat_axis=0, tiled=True)
    attention = finish_attention(*attention_parts)
    migrated_pool = lax.dynamic_update_slice_in_dim(
        written,
        arrived.reshape((homes * capacity,) + key_value_pages.shape[1:]),
        live_slots,
        axis=0,
    )
    return (attention, migrated_pool)


def solution(mesh):
    in_specs = (
        P(None, "req"),
        P("req", "grp"),
        P("req", "grp", None),
        P(None, None, "grp"),
        P(),
        P("req", None),
        P("req", "grp", None, None, None),
        P("req"),
        P("req", None),
        P("req"),
        P("req", None),
    )
    out_specs = (P("req", None), P("req", "grp", None, None, None))
    return jax.shard_map(shards, mesh=mesh, in_specs=in_specs, out_specs=out_specs, check_vma=False)
```

```python
import math

import jax
import jax.numpy as jnp
from jax import lax
from jax.sharding import PartitionSpec as P

adapter_scale = 2.0
masked_score = -1e30


def split_three(value):
    first = lax.reduce_precision(value, exponent_bits=8, mantissa_bits=7)
    rest = value - first
    second = lax.reduce_precision(rest, exponent_bits=8, mantissa_bits=7)
    third = rest - second
    return jnp.concatenate([first, second, third], axis=-1).astype(jnp.bfloat16)


def join_three(parts, width):
    wide = parts.astype(jnp.float32)
    return wide[..., :width] + wide[..., width : 2 * width] + wide[..., 2 * width :]


def finish_attention(all_mixed, all_top, all_total, query, new_keys, new_values):
    rows, heads, group_size, head_dim = query.shape
    new_score = jnp.einsum(
        "ihgd,hid->hgi", query, new_keys, preferred_element_type=jnp.float32
    ) / math.sqrt(head_dim)
    top = jnp.maximum(all_top, new_score)
    old_scale = jnp.exp(all_top - top)
    new_weight = jnp.exp(new_score - top)
    total = all_total * old_scale + new_weight
    mixed = (
        all_mixed * old_scale[..., None]
        + new_weight[..., None] * new_values.astype(jnp.float32)[:, None, :, :]
    )
    attention = (mixed / total[..., None]).astype(jnp.bfloat16)
    return attention.transpose(2, 0, 1, 3).reshape(rows, -1)

def shards(
    normed_token_input,
    key_value_weight,
    adapter_down_weight,
    adapter_up_weight,
    adapter_index_rows,
    queries,
    key_value_pages,
    lengths,
    page_slot_table,
    departing_slots,
    departing_target,
):
    selected_adapter = adapter_index_rows[:, 0]
    request_index = jnp.arange(lengths.shape[0], dtype=jnp.int32)
    homes = lax.axis_size("req")
    groups = lax.axis_size("grp")
    home_index = lax.axis_index("req")
    group_index = lax.axis_index("grp")
    rows = lengths.shape[0]
    request_count = normed_token_input.shape[0]
    column_span = key_value_weight.shape[1]
    local_adapters = adapter_down_weight.shape[1]
    rank_width = adapter_down_weight.shape[2]
    rank_half = adapter_up_weight.shape[1]
    slot_tokens = key_value_pages.shape[1]
    heads = key_value_pages.shape[3]
    head_dim = key_value_pages.shape[4]
    key_width = heads * head_dim
    query_heads = queries.shape[1] // head_dim
    heads_per_target = query_heads // groups
    page_size = slot_tokens * groups
    pages = page_slot_table.shape[1]

    both = jnp.concatenate(
        [key_value_weight, adapter_down_weight.reshape(adapter_down_weight.shape[0], -1)], axis=1
    )
    products = jnp.dot(normed_token_input, both, preferred_element_type=jnp.float32).reshape(
        homes, rows, -1
    )
    base_part = products[:, :, :column_span]
    down_all = products[:, :, column_span:].reshape(homes, rows, local_adapters, rank_width)
    local_choice = (selected_adapter - group_index * local_adapters).reshape(homes, rows)
    picker = local_choice[:, :, None] == jnp.arange(local_adapters, dtype=jnp.int32)[None, None, :]
    mid_part = jnp.sum(jnp.where(picker[..., None], down_all, 0.0), axis=2)
    partial = jnp.concatenate([base_part, mid_part], axis=2)
    resident_adapters = lax.dynamic_slice_in_dim(selected_adapter, home_index * rows, rows)
    up_weight_rows = adapter_up_weight[resident_adapters]
    summed = jnp.sum(lax.all_to_all(partial, "req", 0, 0, tiled=False), axis=0)
    base_resident = summed[:, :column_span]

    owner = resident_adapters // local_adapters
    is_value = group_index * column_span >= key_width

    live_slots = rows * pages
    live = key_value_pages[:live_slots, 0]
    keys = live[:, 0]
    values = live[:, 1]
    query = queries.reshape(rows, heads, -1, head_dim)
    group_size = query.shape[2]
    entry_of_slot = jnp.argmax(
        page_slot_table.reshape(1, -1) == jnp.arange(live_slots, dtype=jnp.int32)[:, None], axis=1
    )
    slot_request = entry_of_slot // pages
    slot_position = (entry_of_slot % pages) * page_size + group_index * slot_tokens
    valid = (slot_request[None, :] == request_index[:, None]) & (
        slot_position[None, :] < lengths[:, None]
    )
    valid = valid[None, None]
    scores = jnp.einsum(
        "ihgd,shd->hgis", query, keys, preferred_element_type=jnp.float32
    ) / math.sqrt(head_dim)
    scores = jnp.where(valid, scores, masked_score)
    local_top = jnp.max(scores, axis=3)
    weights = jnp.where(valid, jnp.exp(scores - local_top[..., None]), 0.0)
    local_total = jnp.sum(weights, axis=3)
    local_mixed = jnp.einsum(
        "hgis,shd->hgid", weights, values, preferred_element_type=jnp.float32
    )

    block_rows = heads_per_target * rows
    stat_count = heads_per_target * rows
    stat_rows = -(-6 * stat_count // head_dim)
    spare_rows = 8 - stat_rows
    stats = jnp.concatenate(
        [local_top.reshape(groups, stat_count), local_total.reshape(groups, stat_count)], axis=1
    )
    stat_pack = jnp.concatenate(
        [split_three(stats), jnp.zeros((groups, stat_rows * head_dim - 6 * stat_count), jnp.bfloat16)],
        axis=1,
    ).reshape(groups, stat_rows, head_dim)
    mid_rows = summed[:, column_span:].astype(jnp.bfloat16)
    parcel = jnp.concatenate(
        [
            local_mixed.reshape(groups, block_rows, head_dim).astype(jnp.bfloat16),
            jnp.broadcast_to(mid_rows[None], (groups,) + mid_rows.shape),
            stat_pack,
            jnp.zeros((groups, spare_rows, head_dim), jnp.bfloat16),
        ],
        axis=1,
    )
    received, up_weight_rows, departing_slots, departing_target = lax.optimization_barrier(
        (
            lax.all_to_all(parcel, "grp", 0, 0, tiled=False),
            up_weight_rows,
            departing_slots,
            departing_target,
        )
    )
    stat_at = block_rows + rows
    shard_mixed = received[:, :block_rows].astype(jnp.float32).reshape(
        groups, heads_per_target, rows, head_dim
    )
    shard_stats = join_three(
        received[:, stat_at : stat_at + stat_rows].reshape(groups, -1)[:, : 6 * stat_count],
        2 * stat_count,
    )
    shard_top = shard_stats[:, :stat_count].reshape(groups, heads_per_target, rows)
    shard_total = shard_stats[:, stat_count:].reshape(groups, heads_per_target, rows)
    mid_spread = received[:, block_rows:stat_at]
    top_own = jnp.max(shard_top, axis=0)
    shard_scale = jnp.exp(shard_top - top_own[None])
    total_own = jnp.sum(shard_total * shard_scale, axis=0)
    mixed_own = jnp.sum(shard_mixed * shard_scale[..., None], axis=0)

    from_owner = owner[None, :, None] == jnp.arange(groups, dtype=jnp.int32)[:, None, None]
    mid_home = jnp.sum(
        jnp.where(from_owner, mid_spread.astype(jnp.float32), 0.0), axis=0
    ).astype(jnp.bfloat16)
    mid_used = jnp.where(is_value, mid_home[:, rank_half:], mid_home[:, :rank_half])
    adapter_update = jnp.einsum(
        "ir,irc->ic", mid_used, up_weight_rows, preferred_element_type=jnp.float32
    )
    fresh_columns = (base_resident + adapter_scale * adapter_update).astype(jnp.bfloat16)

    own_stats = jnp.concatenate(
        [top_own.reshape(1, stat_count), total_own.reshape(1, stat_count)], axis=1
    )
    merged = jnp.concatenate(
        [
            mixed_own.reshape(block_rows, head_dim).astype(jnp.bfloat16),
            fresh_columns,
            jnp.concatenate(
                [
                    split_three(own_stats),
                    jnp.zeros((1, stat_rows * head_dim - 6 * stat_count), jnp.bfloat16),
                ],
                axis=1,
            ).reshape(stat_rows, head_dim),
            jnp.zeros((spare_rows, head_dim), jnp.bfloat16),
        ],
        axis=0,
    )
    everything = lax.all_to_all(
        jnp.broadcast_to(merged[None], (groups,) + merged.shape), "grp", 0, 0, tiled=False
    )
    all_mixed = everything[:, :block_rows].astype(jnp.float32).reshape(
        heads, group_size, rows, head_dim
    )
    all_stats = join_three(
        everything[:, stat_at : stat_at + stat_rows].reshape(groups, -1)[:, : 6 * stat_count],
        2 * stat_count,
    )
    all_top = all_stats[:, :stat_count].reshape(heads, group_size, rows)
    all_total = all_stats[:, stat_count:].reshape(heads, group_size, rows)
    new_all = everything[:, block_rows:stat_at]
    new_keys = new_all[: groups // 2]
    new_values = new_all[groups // 2 :]
    attention_parts = (all_mixed, all_top, all_total, query, new_keys, new_values)

    targets = departing_target[:, 0]
    count_out = departing_slots.shape[0]
    order = jnp.arange(count_out, dtype=jnp.int32)
    earlier = (targets[:, None] == targets[None, :]) & (order[None, :] < order[:, None])
    place = jnp.sum(earlier.astype(jnp.int32), axis=1)
    live_slots = rows * pages
    capacity = (key_value_pages.shape[0] - live_slots) // homes
    lands = (targets[None, None, :] == jnp.arange(homes, dtype=jnp.int32)[:, None, None]) & (
        place[None, None, :] == jnp.arange(capacity, dtype=jnp.int32)[None, :, None]
    )
    filled = jnp.any(lands, axis=2)
    source_slot = jnp.sum(jnp.where(lands, departing_slots[None, None, :], 0), axis=2)

    page_slot = page_slot_table[request_index, lengths // page_size]
    offset = lengths % page_size
    mine = offset // slot_tokens == group_index
    token_local = offset % slot_tokens
    current = key_value_pages[page_slot, token_local]
    fresh = jnp.stack([new_keys, new_values], axis=0).transpose(2, 0, 1, 3)
    written = key_value_pages.at[page_slot, token_local].set(
        jnp.where(mine[:, None, None, None], fresh, current)
    )

    written = written.at[live_slots].set(jnp.zeros((), key_value_pages.dtype))
    outbound = written[jnp.where(filled, source_slot, live_slots)]
    outbound, attention_parts = lax.optimization_barrier((outbound, attention_parts))
    arrived = lax.all_to_all(outbound, "req", split_axis=0, concat_axis=0, tiled=True)
    attention = finish_attention(*attention_parts)
    migrated_pool = lax.dynamic_update_slice_in_dim(
        written,
        arrived.reshape((homes * capacity,) + key_value_pages.shape[1:]),
        live_slots,
        axis=0,
    )
    return (attention, migrated_pool)


def solution(mesh):
    in_specs = (
        P(None, "req"),
        P("req", "grp"),
        P("req", "grp", None),
        P(None, None, "grp"),
        P(),
        P("req", None),
        P("req", "grp", None, None, None),
        P("req"),
        P("req", None),
        P("req"),
        P("req", None),
    )
    out_specs = (P("req", None), P("req", "grp", None, None, None))
    return jax.shard_map(shards, mesh=mesh, in_specs=in_specs, out_specs=out_specs, check_vma=False)
```
